512 devices in a mesh: aux: 8 (over y), ao: 64 (over x, z, core).
Axes of the slice: x: 4, y: 8, z: 8, core: 2. Of those that a mesh axis runs over, the one named last changes fastest.
Arguments:
- pair_list: int32 [1536, 2], P('ao'), may hold values from 0 to 255, as said below
- pair_count: int32 [64], P('ao'), may hold values from 3 to 24, as said below
- tiles: bfloat16 [1536, 32, 128, 128], P('ao', 'aux'), may hold values from -6 to 6
- coeff: bfloat16 [32768, 512], P('ao'), may hold values from -0.25 to 0.25
Outputs:
- k_tiles: bfloat16 [1536, 128, 128], P('ao', 'aux')
The draws below stay inside these ranges and needn't reach their ends.
Inputs may be any that keep to these rules, and one draw needn't show every extreme that they name: `pair_list`: each live row of owner o names i among its blocks and i < j < (o + 3) * 4; no live pair repeats; rows past an owner's count repeat that owner's first row. `pair_count`: some owner has exactly 24 live rows.
All inputs are finite; a program needn't handle non-finite values.
Results may differ from the reference program's by a relative error of at most 0.0067.
Values may be sent and summed in bfloat16 or wider, within the bound.
No kernel may reach another device: no remote copies, remote signals or barrier semaphores. Data moves between devices by JAX's collectives and lax.ppermute only.
A program may use at most 64 MiB of HBM per device.

```python
import jax
import jax.numpy as jnp
from jax import lax

BLK = 128
OCC = 512
NB_DEV = 4
BAND = 2
PAIR_DEV = 24
AUX = 32
NAO = 32768
PAIRS = 1536
N_AO = 64


def pair_plan(key):
    block_total = N_AO * NB_DEV
    window_blocks = (BAND + 1) * NB_DEV
    option_total = NB_DEV * window_blocks
    base_key = jax.random.fold_in(key, 11)
    score_key, shrink_key, fullest_key = jax.random.split(base_key, 3)
    owner_index = jnp.arange(N_AO, dtype=jnp.int32)[:, None]
    option = jnp.arange(option_total, dtype=jnp.int32)[None, :]
    left_pick = option // window_blocks
    right_pick = option % window_blocks
    usable = (right_pick > left_pick) & (owner_index * NB_DEV + right_pick < block_total)
    scores = jax.random.randint(score_key, (N_AO, option_total), 0, 1 << 20) * option_total + option
    scores = scores + jnp.where(usable, 0, 1 << 27).astype(jnp.int32)
    ranking = jnp.argsort(scores, axis=1)[:, :PAIR_DEV].astype(jnp.int32)
    chosen_left = ranking // window_blocks
    chosen_right = ranking % window_blocks
    shrink = jax.random.randint(shrink_key, (N_AO,), 0, 4)
    live_count = jnp.maximum(1, PAIR_DEV // jnp.left_shift(jnp.ones_like(shrink), shrink))
    fullest = jax.random.randint(fullest_key, (), 0, N_AO - BAND)
    live_count = jnp.where(owner_index[:, 0] == fullest, PAIR_DEV, live_count)
    live_count = jnp.minimum(live_count, jnp.sum(usable.astype(jnp.int32), axis=1))
    slot_index = jnp.arange(PAIR_DEV, dtype=jnp.int32)[None, :]
    keep = slot_index < live_count[:, None]
    chosen_left = jnp.where(keep, chosen_left, chosen_left[:, :1])
    chosen_right = jnp.where(keep, chosen_right, chosen_right[:, :1])
    left_block = owner_index * NB_DEV + chosen_left
    right_block = owner_index * NB_DEV + chosen_right
    pair_rows = jnp.stack([left_block, right_block], -1).reshape(N_AO * PAIR_DEV, 2).astype(jnp.int32)
    return (pair_rows, live_count.astype(jnp.int32))


def draw_pair_list(key, part):
    pair_rows, live_count = pair_plan(key)
    return pair_rows


def draw_pair_count(key, part):
    pair_rows, live_count = pair_plan(key)
    return live_count


def shard_levels(stream_key, shape, cuts, least, top_value):
    def one(dim, parts):
        steps = jax.random.uniform(jax.random.fold_in(jax.random.fold_in(stream_key, 6), dim), (parts,), jnp.float32, least / len(cuts), top_value / len(cuts))
        return jnp.repeat(jnp.exp(steps), shape[dim] // parts).reshape((-1,) + (1,) * (len(shape) - dim - 1))

    gain = one(*cuts[0])
    for cut in cuts[1:]:
        gain = gain * one(*cut)
    return gain


def noise(stream_key, dims, deviation, limit, cuts=(), kind=jnp.bfloat16):
    factor_of = shard_levels(stream_key, dims, cuts, -0.22, 0.18) if cuts else 1.0
    drawn = jax.random.normal(stream_key, dims, jnp.float32) * deviation * factor_of
    return jnp.minimum(jnp.maximum(drawn, -limit), limit).astype(kind)


def setup_inputs(seed: int = 0) -> dict:
    key_list = jax.random.split(jax.random.key(seed), 5)
    pair_list = draw_pair_list(jax.random.fold_in(key_list[4], 71), 0)
    pair_count = draw_pair_count(jax.random.fold_in(key_list[4], 71), 0)
    tiles = noise(key_list[2], (PAIRS, AUX, BLK, BLK), 1.0, 6.0, ((0, 64), (1, 8)))
    coeff = noise(key_list[3], (NAO, OCC), (BLK * 5) ** -0.5, 0.25, ((0, 64),))
    return dict(pair_list=pair_list, pair_count=pair_count, tiles=tiles, coeff=coeff)


def reference(pair_list, pair_count, tiles, coeff):
    block_total = N_AO * NB_DEV
    window_blocks = (BAND + 1) * NB_DEV
    blocks = coeff.reshape(block_total, BLK, OCC)
    padded = jnp.concatenate([blocks, jnp.zeros((BAND * NB_DEV, BLK, OCC), blocks.dtype)], 0)
    pair_rows = pair_list.reshape(N_AO, PAIR_DEV, 2)
    grouped = tiles.reshape(N_AO, PAIR_DEV, AUX, BLK, BLK)

    def owner_step(running, inputs):
        owner_index, owner_pairs, live_count, owner_tiles = inputs
        first_block = owner_index * NB_DEV
        window = lax.dynamic_slice_in_dim(padded, first_block, window_blocks, 0).astype(jnp.float32)

        def add_pair(slot_index, totals):
            left_block = (owner_pairs[slot_index, 0] - first_block).astype(jnp.int32)
            right_block = (owner_pairs[slot_index, 1] - first_block).astype(jnp.int32)
            is_live = slot_index < live_count
            pair_tile = owner_tiles[slot_index].astype(jnp.float32)
            to_left = jnp.einsum("pmn,nk->pmk", pair_tile, window[right_block])
            to_right = jnp.einsum("pmn,mk->pnk", pair_tile, window[left_block])
            nothing = jnp.zeros_like(to_left)
            totals = totals.at[left_block].add(jnp.where(is_live, to_left, nothing))
            return totals.at[right_block].add(jnp.where(is_live, to_right, nothing))

        totals = lax.fori_loop(0, PAIR_DEV, add_pair, jnp.zeros((window_blocks, AUX, BLK, OCC), jnp.float32))
        halves = lax.optimization_barrier(totals.astype(jnp.bfloat16)).astype(jnp.float32)
        running = running + halves
        finished = running[:NB_DEV].astype(jnp.bfloat16)
        running = jnp.concatenate([running[NB_DEV:], jnp.zeros((NB_DEV, AUX, BLK, OCC), jnp.float32)], 0)
        return running, finished

    owners = jnp.arange(N_AO, dtype=jnp.int32)
    start = jnp.zeros((window_blocks, AUX, BLK, OCC), jnp.float32)
    _, fitted = lax.scan(owner_step, start, (owners, pair_rows, pair_count, grouped))
    fitted = fitted.reshape(block_total, AUX, BLK, OCC)
    norm_factor = (AUX * OCC) ** -0.5
    slot_ids = jnp.arange(N_AO * PAIR_DEV, dtype=jnp.int32)
    flat_live = (slot_ids % PAIR_DEV) < jnp.repeat(pair_count, PAIR_DEV)

    def contract(entry_pair):
        pair_row, is_live = entry_pair
        left_rows = fitted[pair_row[0]].astype(jnp.float32)
        right_rows = fitted[pair_row[1]].astype(jnp.float32)
        pair_tile = jnp.einsum("pmk,pnk->mn", left_rows, right_rows) * norm_factor
        return jnp.where(is_live, pair_tile, jnp.zeros_like(pair_tile)).astype(jnp.bfloat16)

    return lax.map(contract, (pair_list, flat_live))
```

```python
import jax
import jax.numpy as jnp
from jax import lax
from jax.experimental import pallas as pl
from jax.experimental.pallas import tpu as pltpu
from jax.sharding import PartitionSpec as P

BAND = 2


def passed_along(value, axis, steps):
    count = lax.axis_size(axis)
    first, last = (max(0, -steps), min(count, count - steps))
    return lax.ppermute(value, axis, [(source, source + steps) for source in range(first, last)])


def _half_kernel(left_ref, right_ref, count_ref, tile_ref, coeff_ref, out_ref, acc_ref):
    slot = pl.program_id(0)

    @pl.when(slot == 0)
    def _():
        acc_ref[...] = jnp.zeros_like(acc_ref)

    @pl.when(slot < count_ref[0])
    def _():
        left = left_ref[slot]
        right = right_ref[slot]
        tile = tile_ref[0]
        aux_local, block_size, _ = tile.shape
        right_coeff = coeff_ref[right]
        left_coeff = coeff_ref[left]
        to_left = jnp.dot(
            tile.reshape(aux_local * block_size, block_size),
            right_coeff,
            preferred_element_type=jnp.float32,
        ).reshape(aux_local, block_size, -1)
        acc_ref[left] += to_left
        parts = [
            lax.dot_general(
                tile[p], left_coeff, (((0,), (0,)), ((), ())),
                preferred_element_type=jnp.float32,
            )
            for p in range(aux_local)
        ]
        acc_ref[right] += jnp.stack(parts, 0)

    @pl.when(slot == pl.num_programs(0) - 1)
    def _():
        out_ref[...] = acc_ref[...].astype(out_ref.dtype)


def _contract_kernel(left_ref, right_ref, count_ref, fitted_ref, out_ref):
    slot = pl.program_id(0)
    live = slot < count_ref[0]

    @pl.when(live)
    def _():
        left_rows = fitted_ref[left_ref[slot]]
        right_rows = fitted_ref[right_ref[slot]]
        total = None
        for p in range(left_rows.shape[0]):
            part = lax.dot_general(
                left_rows[p], right_rows[p], (((1,), (1,)), ((), ())),
                preferred_element_type=jnp.float32,
            )
            total = part if total is None else total + part
        out_ref[0] = total

    @pl.when(jnp.logical_not(live))
    def _():
        out_ref[...] = jnp.zeros_like(out_ref)


def on_device(pair_list, pair_count, tiles, coeff):
    pair_slots = pair_list.shape[0]
    aux_local = tiles.shape[1]
    block_size = tiles.shape[2]
    orbitals = coeff.shape[1]
    own_blocks = coeff.shape[0] // block_size
    window_blocks = (BAND + 1) * own_blocks
    owner_index = lax.axis_index("ao")
    first_block = owner_index * own_blocks
    left_rel = (pair_list[:, 0] - first_block).astype(jnp.int32)
    right_rel = (pair_list[:, 1] - first_block).astype(jnp.int32)
    count = pair_count.astype(jnp.int32)
    own_coeff = coeff.reshape(own_blocks, block_size, orbitals)
    ahead_coeff = [passed_along(own_coeff, "ao", -distance) for distance in range(1, BAND + 1)]
    window_coeff = jnp.concatenate([own_coeff] + ahead_coeff, 0)

    def tile_map(slot, left, right, cnt):
        return (jnp.minimum(slot, jnp.maximum(cnt[0] - 1, 0)), 0, 0, 0)

    halves = pl.pallas_call(
        _half_kernel,
        grid_spec=pltpu.PrefetchScalarGridSpec(
            num_scalar_prefetch=3,
            grid=(pair_slots,),
            in_specs=[
                pl.BlockSpec((1, aux_local, block_size, block_size), tile_map),
                pl.BlockSpec(
                    (window_blocks, block_size, orbitals), lambda s, l, r, c: (0, 0, 0)
                ),
            ],
            out_specs=pl.BlockSpec(
                (window_blocks, aux_local, block_size, orbitals),
                lambda s, l, r, c: (0, 0, 0, 0),
            ),
            scratch_shapes=[
                pltpu.VMEM((window_blocks, aux_local, block_size, orbitals), jnp.float32)
            ],
        ),
        out_shape=jax.ShapeDtypeStruct(
            (window_blocks, aux_local, block_size, orbitals), jnp.bfloat16
        ),
        compiler_params=pltpu.CompilerParams(
            dimension_semantics=("arbitrary",), vmem_limit_bytes=48 * 1024 * 1024
        ),
    )(left_rel, right_rel, count, tiles, window_coeff)

    fitted_sum = halves[:own_blocks].astype(jnp.float32)
    for distance in range(1, BAND + 1):
        outgoing = halves[distance * own_blocks : (distance + 1) * own_blocks]
        arriving = passed_along(outgoing, "ao", distance)
        fitted_sum = fitted_sum + arriving.astype(jnp.float32)
    fitted = fitted_sum.astype(jnp.bfloat16)
    ahead_fitted = [passed_along(fitted, "ao", -distance) for distance in range(1, BAND + 1)]
    window_fitted = jnp.concatenate([fitted] + ahead_fitted, 0)

    partial_tiles = pl.pallas_call(
        _contract_kernel,
        grid_spec=pltpu.PrefetchScalarGridSpec(
            num_scalar_prefetch=3,
            grid=(pair_slots,),
            in_specs=[
                pl.BlockSpec(
                    (window_blocks, aux_local, block_size, orbitals),
                    lambda s, l, r, c: (0, 0, 0, 0),
                ),
            ],
            out_specs=pl.BlockSpec((1, block_size, block_size), lambda s, l, r, c: (s, 0, 0)),
        ),
        out_shape=jax.ShapeDtypeStruct((pair_slots, block_size, block_size), jnp.float32),
        compiler_params=pltpu.CompilerParams(
            dimension_semantics=("arbitrary",), vmem_limit_bytes=48 * 1024 * 1024
        ),
    )(left_rel, right_rel, count, window_fitted)

    summed = lax.psum_scatter(partial_tiles, "aux", scatter_dimension=1, tiled=True)
    norm_factor = (aux_local * lax.axis_size("aux") * orbitals) ** (-0.5)
    return (summed * norm_factor).astype(jnp.bfloat16)


def solution(mesh):
    in_specs = (P("ao", None), P("ao"), P("ao", "aux", None, None), P("ao", None))
    out_specs = P("ao", "aux", None)
    return jax.shard_map(
        on_device, mesh=mesh, in_specs=in_specs, out_specs=out_specs, check_vma=False
    )
```

```python
import jax
import jax.numpy as jnp
from jax import lax
from jax.experimental import pallas as pl
from jax.experimental.pallas import tpu as pltpu
from jax.sharding import PartitionSpec as P

BAND = 2


def passed_along(value, axis, steps):
    count = lax.axis_size(axis)
    first, last = (max(0, -steps), min(count, count - steps))
    return lax.ppermute(value, axis, [(source, source + steps) for source in range(first, last)])


def _half_kernel(left_ref, right_ref, count_ref, tile_ref, coeff_ref, out_ref, acc_ref):
    slot = pl.program_id(0)

    @pl.when(slot == 0)
    def _():
        acc_ref[...] = jnp.zeros_like(acc_ref)

    @pl.when(slot < count_ref[0])
    def _():
        left = left_ref[slot]
        right = right_ref[slot]
        tile = tile_ref[0]
        aux_local, block_size, _ = tile.shape
        right_coeff = coeff_ref[right]
        left_coeff = coeff_ref[left]
        to_left = jnp.dot(
            tile.reshape(aux_local * block_size, block_size),
            right_coeff,
            preferred_element_type=jnp.float32,
        ).reshape(aux_local, block_size, -1)
        acc_ref[left] += to_left
        parts = [
            lax.dot_general(
                tile[p], left_coeff, (((0,), (0,)), ((), ())),
                preferred_element_type=jnp.float32,
            )
            for p in range(aux_local)
        ]
        acc_ref[right] += jnp.stack(parts, 0)

    @pl.when(slot == pl.num_programs(0) - 1)
    def _():
        chunks = out_ref.shape[0]
        width = out_ref.shape[-1]
        for c in range(chunks):
            out_ref[c] = acc_ref[:, :, :, c * width : (c + 1) * width].astype(out_ref.dtype)


def _contract_kernel(left_ref, right_ref, count_ref, own_ref, near_ref, far_ref, prev_ref, out_ref):
    slot = pl.program_id(0)
    live = slot < count_ref[0]
    own_blocks = own_ref.shape[0]

    @pl.when(live)
    def _():
        left_rows = own_ref[left_ref[slot]]
        right = right_ref[slot]
        group = right // own_blocks
        index = right % own_blocks
        right_rows = jnp.where(
            group == 0, own_ref[index], jnp.where(group == 1, near_ref[index], far_ref[index])
        )
        total = prev_ref[0]
        for p in range(left_rows.shape[0]):
            total = total + lax.dot_general(
                left_rows[p], right_rows[p], (((1,), (1,)), ((), ())),
                preferred_element_type=jnp.float32,
            )
        out_ref[0] = total

    @pl.when(jnp.logical_not(live))
    def _():
        out_ref[...] = jnp.zeros_like(out_ref)


CHUNKS = 4


def on_device(pair_list, pair_count, tiles, coeff):
    pair_slots = pair_list.shape[0]
    aux_local = tiles.shape[1]
    block_size = tiles.shape[2]
    orbitals = coeff.shape[1]
    own_blocks = coeff.shape[0] // block_size
    window_blocks = (BAND + 1) * own_blocks
    width = orbitals // CHUNKS
    devices = lax.axis_size("ao")
    owner_index = lax.axis_index("ao")
    first_block = owner_index * own_blocks
    left_rel = (pair_list[:, 0] - first_block).astype(jnp.int32)
    right_rel = (pair_list[:, 1] - first_block).astype(jnp.int32)
    count = pair_count.astype(jnp.int32)
    own_coeff = coeff.reshape(own_blocks, block_size, orbitals)
    ahead_coeff = [passed_along(own_coeff, "ao", -distance) for distance in range(1, BAND + 1)]
    window_coeff = jnp.concatenate([own_coeff] + ahead_coeff, 0)

    def tile_map(slot, left, right, cnt):
        return (jnp.minimum(slot, jnp.maximum(cnt[0] - 1, 0)), 0, 0, 0)

    halves = pl.pallas_call(
        _half_kernel,
        grid_spec=pltpu.PrefetchScalarGridSpec(
            num_scalar_prefetch=3,
            grid=(pair_slots,),
            in_specs=[
                pl.BlockSpec((1, aux_local, block_size, block_size), tile_map),
                pl.BlockSpec(
                    (window_blocks, block_size, orbitals), lambda s, l, r, c: (0, 0, 0)
                ),
            ],
            out_specs=pl.BlockSpec(
                (CHUNKS, window_blocks, aux_local, block_size, width),
                lambda s, l, r, c: (0, 0, 0, 0, 0),
            ),
            scratch_shapes=[
                pltpu.VMEM((window_blocks, aux_local, block_size, orbitals), jnp.float32)
            ],
        ),
        out_shape=jax.ShapeDtypeStruct(
            (CHUNKS, window_blocks, aux_local, block_size, width), jnp.bfloat16
        ),
        compiler_params=pltpu.CompilerParams(
            dimension_semantics=("arbitrary",), vmem_limit_bytes=48 * 1024 * 1024
        ),
    )(left_rel, right_rel, count, tiles, window_coeff)

    odd_down_one = [(s, s - 1) for s in range(1, devices, 2)]
    odd_down_two = [(s, s - 2) for s in range(3, devices, 2)]
    is_even = (owner_index % 2) == 0
    block_shape = (own_blocks, aux_local, block_size, width)
    partial_tiles = jnp.zeros((pair_slots, block_size, block_size), jnp.float32)
    pending = halves[0]
    for c in range(CHUNKS):
        chunk = pending
        from_one = passed_along(chunk[own_blocks : 2 * own_blocks], "ao", 1)
        from_two = passed_along(chunk[2 * own_blocks :], "ao", 2)
        fitted = (
            (from_two.astype(jnp.float32) + from_one.astype(jnp.float32))
            + chunk[:own_blocks].astype(jnp.float32)
        ).astype(jnp.bfloat16)
        if c + 1 < CHUNKS:
            fitted, pending = lax.optimization_barrier((fitted, halves[c + 1]))
        near = passed_along(fitted, "ao", -1)
        relayed = lax.ppermute(near, "ao", odd_down_one)
        direct = lax.ppermute(fitted, "ao", odd_down_two)
        far = jnp.where(is_even, relayed, direct)
        partial_tiles = pl.pallas_call(
            _contract_kernel,
            grid_spec=pltpu.PrefetchScalarGridSpec(
                num_scalar_prefetch=3,
                grid=(pair_slots,),
                in_specs=[
                    pl.BlockSpec(block_shape, lambda s, l, r, n: (0, 0, 0, 0)),
                    pl.BlockSpec(block_shape, lambda s, l, r, n: (0, 0, 0, 0)),
                    pl.BlockSpec(block_shape, lambda s, l, r, n: (0, 0, 0, 0)),
                    pl.BlockSpec((1, block_size, block_size), lambda s, l, r, n: (s, 0, 0)),
                ],
                out_specs=pl.BlockSpec(
                    (1, block_size, block_size), lambda s, l, r, n: (s, 0, 0)
                ),
            ),
            out_shape=jax.ShapeDtypeStruct((pair_slots, block_size, block_size), jnp.float32),
            input_output_aliases={6: 0},
            compiler_params=pltpu.CompilerParams(dimension_semantics=("arbitrary",)),
        )(left_rel, right_rel, count, fitted, near, far, partial_tiles)

    summed = lax.psum_scatter(partial_tiles, "aux", scatter_dimension=1, tiled=True)
    norm_factor = (aux_local * lax.axis_size("aux") * orbitals) ** (-0.5)
    return (summed * norm_factor).astype(jnp.bfloat16)


def solution(mesh):
    in_specs = (P("ao", None), P("ao"), P("ao", "aux", None, None), P("ao", None))
    out_specs = P("ao", "aux", None)
    return jax.shard_map(
        on_device, mesh=mesh, in_specs=in_specs, out_specs=out_specs, check_vma=False
    )
```

```python
import jax
import jax.numpy as jnp
from jax import lax
from jax.experimental import pallas as pl
from jax.experimental.pallas import tpu as pltpu
from jax.sharding import PartitionSpec as P

BAND = 2


def passed_along(value, axis, steps):
    count = lax.axis_size(axis)
    first, last = (max(0, -steps), min(count, count - steps))
    return lax.ppermute(value, axis, [(source, source + steps) for source in range(first, last)])


def _half_kernel(left_ref, right_ref, count_ref, tile_ref, coeff_ref, out_ref, acc_ref):
    slot = pl.program_id(0)

    @pl.when(slot == 0)
    def _():
        acc_ref[...] = jnp.zeros_like(acc_ref)

    @pl.when(slot < count_ref[0])
    def _():
        left = left_ref[slot]
        right = right_ref[slot]
        tile = tile_ref[0]
        aux_local, block_size, _ = tile.shape
        right_coeff = coeff_ref[right]
        left_coeff = coeff_ref[left]
        to_left = jnp.dot(
            tile.reshape(aux_local * block_size, block_size),
            right_coeff,
            preferred_element_type=jnp.float32,
        ).reshape(aux_local, block_size, -1)
        acc_ref[left] += to_left
        parts = [
            lax.dot_general(
                tile[p], left_coeff, (((0,), (0,)), ((), ())),
                preferred_element_type=jnp.float32,
            )
            for p in range(aux_local)
        ]
        acc_ref[right] += jnp.stack(parts, 0)

    @pl.when(slot == pl.num_programs(0) - 1)
    def _():
        chunks = out_ref.shape[0]
        width = out_ref.shape[-1]
        for c in range(chunks):
            out_ref[c] = acc_ref[:, :, :, c * width : (c + 1) * width].astype(out_ref.dtype)


def _contract_kernel(left_ref, right_ref, count_ref, *refs):
    out_ref = refs[-1]
    groups = refs[:-1]
    chunks = len(groups) // 3
    slot = pl.program_id(0)
    live = slot < count_ref[0]
    own_blocks = groups[0].shape[0]

    @pl.when(live)
    def _():
        left = left_ref[slot]
        right = right_ref[slot]
        group = right // own_blocks
        index = right % own_blocks
        total = None
        for c in range(chunks):
            own_ref, near_ref, far_ref = groups[3 * c : 3 * c + 3]
            left_rows = own_ref[left]
            right_rows = jnp.where(
                group == 0, own_ref[index], jnp.where(group == 1, near_ref[index], far_ref[index])
            )
            for p in range(left_rows.shape[0]):
                part = lax.dot_general(
                    left_rows[p], right_rows[p], (((1,), (1,)), ((), ())),
                    preferred_element_type=jnp.float32,
                )
                total = part if total is None else total + part
        out_ref[0] = total

    @pl.when(jnp.logical_not(live))
    def _():
        out_ref[...] = jnp.zeros_like(out_ref)


CHUNKS = 4


def on_device(pair_list, pair_count, tiles, coeff):
    pair_slots = pair_list.shape[0]
    aux_local = tiles.shape[1]
    block_size = tiles.shape[2]
    orbitals = coeff.shape[1]
    own_blocks = coeff.shape[0] // block_size
    window_blocks = (BAND + 1) * own_blocks
    width = orbitals // CHUNKS
    devices = lax.axis_size("ao")
    owner_index = lax.axis_index("ao")
    first_block = owner_index * own_blocks
    left_rel = (pair_list[:, 0] - first_block).astype(jnp.int32)
    right_rel = (pair_list[:, 1] - first_block).astype(jnp.int32)
    count = pair_count.astype(jnp.int32)
    own_coeff = coeff.reshape(own_blocks, block_size, orbitals)
    ahead_coeff = [passed_along(own_coeff, "ao", -distance) for distance in range(1, BAND + 1)]
    window_coeff = jnp.concatenate([own_coeff] + ahead_coeff, 0)

    def tile_map(slot, left, right, cnt):
        return (jnp.minimum(slot, jnp.maximum(cnt[0] - 1, 0)), 0, 0, 0)

    halves = pl.pallas_call(
        _half_kernel,
        grid_spec=pltpu.PrefetchScalarGridSpec(
            num_scalar_prefetch=3,
            grid=(pair_slots,),
            in_specs=[
                pl.BlockSpec((1, aux_local, block_size, block_size), tile_map),
                pl.BlockSpec(
                    (window_blocks, block_size, orbitals), lambda s, l, r, c: (0, 0, 0)
                ),
            ],
            out_specs=pl.BlockSpec(
                (CHUNKS, window_blocks, aux_local, block_size, width),
                lambda s, l, r, c: (0, 0, 0, 0, 0),
            ),
            scratch_shapes=[
                pltpu.VMEM((window_blocks, aux_local, block_size, orbitals), jnp.float32)
            ],
        ),
        out_shape=jax.ShapeDtypeStruct(
            (CHUNKS, window_blocks, aux_local, block_size, width), jnp.bfloat16
        ),
        compiler_params=pltpu.CompilerParams(
            dimension_semantics=("arbitrary",), vmem_limit_bytes=48 * 1024 * 1024
        ),
    )(left_rel, right_rel, count, tiles, window_coeff)

    odd_down_one = [(s, s - 1) for s in range(1, devices, 2)]
    odd_down_two = [(s, s - 2) for s in range(3, devices, 2)]
    is_even = (owner_index % 2) == 0
    block_shape = (own_blocks, aux_local, block_size, width)
    pieces = []
    pending = halves[0]
    for c in range(CHUNKS):
        chunk = pending
        from_one = passed_along(chunk[own_blocks : 2 * own_blocks], "ao", 1)
        from_two = passed_along(chunk[2 * own_blocks :], "ao", 2)
        fitted = (
            (from_two.astype(jnp.float32) + from_one.astype(jnp.float32))
            + chunk[:own_blocks].astype(jnp.float32)
        ).astype(jnp.bfloat16)
        if c + 1 < CHUNKS:
            fitted, pending = lax.optimization_barrier((fitted, halves[c + 1]))
        near = passed_along(fitted, "ao", -1)
        relayed = lax.ppermute(near, "ao", odd_down_one)
        direct = lax.ppermute(fitted, "ao", odd_down_two)
        far = jnp.where(is_even, relayed, direct)
        pieces += [fitted, near, far]
    whole = pl.BlockSpec(block_shape, lambda s, l, r, n: (0, 0, 0, 0))
    partial_tiles = pl.pallas_call(
        _contract_kernel,
        grid_spec=pltpu.PrefetchScalarGridSpec(
            num_scalar_prefetch=3,
            grid=(pair_slots,),
            in_specs=[whole] * len(pieces),
            out_specs=pl.BlockSpec((1, block_size, block_size), lambda s, l, r, n: (s, 0, 0)),
        ),
        out_shape=jax.ShapeDtypeStruct((pair_slots, block_size, block_size), jnp.float32),
        compiler_params=pltpu.CompilerParams(
            dimension_semantics=("arbitrary",), vmem_limit_bytes=48 * 1024 * 1024
        ),
    )(left_rel, right_rel, count, *pieces)

    summed = lax.psum_scatter(partial_tiles, "aux", scatter_dimension=1, tiled=True)
    norm_factor = (aux_local * lax.axis_size("aux") * orbitals) ** (-0.5)
    return (summed * norm_factor).astype(jnp.bfloat16)


def solution(mesh):
    in_specs = (P("ao", None), P("ao"), P("ao", "aux", None, None), P("ao", None))
    out_specs = P("ao", "aux", None)
    return jax.shard_map(
        on_device, mesh=mesh, in_specs=in_specs, out_specs=out_specs, check_vma=False
    )
```

```python
import jax
import jax.numpy as jnp
from jax import lax
from jax.experimental import pallas as pl
from jax.experimental.pallas import tpu as pltpu
from jax.sharding import PartitionSpec as P

BAND = 2


def passed_along(value, axis, steps):
    count = lax.axis_size(axis)
    first, last = (max(0, -steps), min(count, count - steps))
    return lax.ppermute(value, axis, [(source, source + steps) for source in range(first, last)])


def _half_kernel(left_ref, right_ref, count_ref, tile_ref, coeff_ref, out_ref, acc_ref):
    slot = pl.program_id(0)

    @pl.when(slot == 0)
    def _():
        acc_ref[...] = jnp.zeros_like(acc_ref)

    @pl.when(slot < count_ref[0])
    def _():
        left = left_ref[slot]
        right = right_ref[slot]
        tile = tile_ref[0]
        aux_local, block_size, _ = tile.shape
        right_coeff = coeff_ref[right]
        left_coeff = coeff_ref[left]
        to_left = jnp.dot(
            tile.reshape(aux_local * block_size, block_size),
            right_coeff,
            preferred_element_type=jnp.float32,
        ).reshape(aux_local, block_size, -1)
        acc_ref[left] += to_left
        parts = [
            lax.dot_general(
                tile[p], left_coeff, (((0,), (0,)), ((), ())),
                preferred_element_type=jnp.float32,
            )
            for p in range(aux_local)
        ]
        acc_ref[right] += jnp.stack(parts, 0)

    @pl.when(slot == pl.num_programs(0) - 1)
    def _():
        chunks = out_ref.shape[0]
        width = out_ref.shape[-1]
        for c in range(chunks):
            out_ref[c] = acc_ref[:, :, :, c * width : (c + 1) * width].astype(out_ref.dtype)


def _contract_kernel(left_ref, right_ref, count_ref, *refs):
    out_ref = refs[-1]
    groups = refs[:-1]
    chunks = len(groups) // 3
    slot = pl.program_id(0)
    live = slot < count_ref[0]
    own_blocks = groups[0].shape[0]

    @pl.when(live)
    def _():
        left = left_ref[slot]
        right = right_ref[slot]
        group = right // own_blocks
        index = right % own_blocks
        total = None
        for c in range(chunks):
            own_ref, near_ref, far_ref = groups[3 * c : 3 * c + 3]
            left_rows = own_ref[left]
            right_rows = jnp.where(
                group == 0, own_ref[index], jnp.where(group == 1, near_ref[index], far_ref[index])
            )
            for p in range(left_rows.shape[0]):
                part = lax.dot_general(
                    left_rows[p], right_rows[p], (((1,), (1,)), ((), ())),
                    preferred_element_type=jnp.float32,
                )
                total = part if total is None else total + part
        out_ref[0] = total

    @pl.when(jnp.logical_not(live))
    def _():
        out_ref[...] = jnp.zeros_like(out_ref)


CHUNKS = 2


def on_device(pair_list, pair_count, tiles, coeff):
    pair_slots = pair_list.shape[0]
    aux_local = tiles.shape[1]
    block_size = tiles.shape[2]
    orbitals = coeff.shape[1]
    own_blocks = coeff.shape[0] // block_size
    window_blocks = (BAND + 1) * own_blocks
    width = orbitals // CHUNKS
    devices = lax.axis_size("ao")
    owner_index = lax.axis_index("ao")
    first_block = owner_index * own_blocks
    left_rel = (pair_list[:, 0] - first_block).astype(jnp.int32)
    right_rel = (pair_list[:, 1] - first_block).astype(jnp.int32)
    count = pair_count.astype(jnp.int32)
    own_coeff = coeff.reshape(own_blocks, block_size, orbitals)
    ahead_coeff = [passed_along(own_coeff, "ao", -distance) for distance in range(1, BAND + 1)]
    window_coeff = jnp.concatenate([own_coeff] + ahead_coeff, 0)

    def tile_map(slot, left, right, cnt):
        return (jnp.minimum(slot, jnp.maximum(cnt[0] - 1, 0)), 0, 0, 0)

    halves = pl.pallas_call(
        _half_kernel,
        grid_spec=pltpu.PrefetchScalarGridSpec(
            num_scalar_prefetch=3,
            grid=(pair_slots,),
            in_specs=[
                pl.BlockSpec((1, aux_local, block_size, block_size), tile_map),
                pl.BlockSpec(
                    (window_blocks, block_size, orbitals), lambda s, l, r, c: (0, 0, 0)
                ),
            ],
            out_specs=pl.BlockSpec(
                (CHUNKS, window_blocks, aux_local, block_size, width),
                lambda s, l, r, c: (0, 0, 0, 0, 0),
            ),
            scratch_shapes=[
                pltpu.VMEM((window_blocks, aux_local, block_size, orbitals), jnp.float32)
            ],
        ),
        out_shape=jax.ShapeDtypeStruct(
            (CHUNKS, window_blocks, aux_local, block_size, width), jnp.bfloat16
        ),
        compiler_params=pltpu.CompilerParams(
            dimension_semantics=("arbitrary",), vmem_limit_bytes=48 * 1024 * 1024
        ),
    )(left_rel, right_rel, count, tiles, window_coeff)

    odd_down_one = [(s, s - 1) for s in range(1, devices, 2)]
    odd_down_two = [(s, s - 2) for s in range(3, devices, 2)]
    is_even = (owner_index % 2) == 0
    block_shape = (own_blocks, aux_local, block_size, width)
    pieces = []
    pending = halves[0]
    for c in range(CHUNKS):
        chunk = pending
        from_one = passed_along(chunk[own_blocks : 2 * own_blocks], "ao", 1)
        from_two = passed_along(chunk[2 * own_blocks :], "ao", 2)
        fitted = (
            (from_two.astype(jnp.float32) + from_one.astype(jnp.float32))
            + chunk[:own_blocks].astype(jnp.float32)
        ).astype(jnp.bfloat16)
        if c + 1 < CHUNKS:
            fitted, pending = lax.optimization_barrier((fitted, halves[c + 1]))
        near = passed_along(fitted, "ao", -1)
        relayed = lax.ppermute(near, "ao", odd_down_one)
        direct = lax.ppermute(fitted, "ao", odd_down_two)
        far = jnp.where(is_even, relayed, direct)
        pieces += [fitted, near, far]
    whole = pl.BlockSpec(block_shape, lambda s, l, r, n: (0, 0, 0, 0))
    partial_tiles = pl.pallas_call(
        _contract_kernel,
        grid_spec=pltpu.PrefetchScalarGridSpec(
            num_scalar_prefetch=3,
            grid=(pair_slots,),
            in_specs=[whole] * len(pieces),
            out_specs=pl.BlockSpec((1, block_size, block_size), lambda s, l, r, n: (s, 0, 0)),
        ),
        out_shape=jax.ShapeDtypeStruct((pair_slots, block_size, block_size), jnp.float32),
        compiler_params=pltpu.CompilerParams(
            dimension_semantics=("arbitrary",), vmem_limit_bytes=48 * 1024 * 1024
        ),
    )(left_rel, right_rel, count, *pieces)

    summed = lax.psum_scatter(partial_tiles, "aux", scatter_dimension=1, tiled=True)
    norm_factor = (aux_local * lax.axis_size("aux") * orbitals) ** (-0.5)
    return (summed * norm_factor).astype(jnp.bfloat16)


def solution(mesh):
    in_specs = (P("ao", None), P("ao"), P("ao", "aux", None, None), P("ao", None))
    out_specs = P("ao", "aux", None)
    return jax.shard_map(
        on_device, mesh=mesh, in_specs=in_specs, out_specs=out_specs, check_vma=False
    )
```

```python
import jax
import jax.numpy as jnp
from jax import lax
from jax.experimental import pallas as pl
from jax.experimental.pallas import tpu as pltpu
from jax.sharding import PartitionSpec as P

BAND = 2


def passed_along(value, axis, steps):
    count = lax.axis_size(axis)
    first, last = (max(0, -steps), min(count, count - steps))
    return lax.ppermute(value, axis, [(source, source + steps) for source in range(first, last)])


def _half_kernel(left_ref, right_ref, count_ref, tile_ref, coeff_ref, out_ref, acc_ref):
    slot = pl.program_id(0)

    @pl.when(slot == 0)
    def _():
        acc_ref[...] = jnp.zeros_like(acc_ref)

    @pl.when(slot < count_ref[0])
    def _():
        left = left_ref[slot]
        right = right_ref[slot]
        tile = tile_ref[0]
        aux_local, block_size, _ = tile.shape
        right_coeff = coeff_ref[right]
        left_coeff = coeff_ref[left]
        to_left = jnp.dot(
            tile.reshape(aux_local * block_size, block_size),
            right_coeff,
            preferred_element_type=jnp.float32,
        ).reshape(aux_local, block_size, -1)
        acc_ref[left] += to_left
        parts = [
            lax.dot_general(
                tile[p], left_coeff, (((0,), (0,)), ((), ())),
                preferred_element_type=jnp.float32,
            )
            for p in range(aux_local)
        ]
        acc_ref[right] += jnp.stack(parts, 0)

    @pl.when(slot == pl.num_programs(0) - 1)
    def _():
        chunks = out_ref.shape[0]
        width = out_ref.shape[-1]
        for c in range(chunks):
            out_ref[c] = acc_ref[:, :, :, c * width : (c + 1) * width].astype(out_ref.dtype)


def _contract_kernel(left_ref, right_ref, count_ref, *refs):
    out_ref = refs[-1]
    groups = refs[:-1]
    chunks = len(groups) // 3
    slot = pl.program_id(0)
    live = slot < count_ref[0]
    own_blocks = groups[0].shape[0]

    @pl.when(live)
    def _():
        left = left_ref[slot]
        right = right_ref[slot]
        group = right // own_blocks
        index = right % own_blocks
        total = None
        for c in range(chunks):
            own_ref, near_ref, far_ref = groups[3 * c : 3 * c + 3]
            left_rows = own_ref[left]
            right_rows = jnp.where(
                group == 0, own_ref[index], jnp.where(group == 1, near_ref[index], far_ref[index])
            )
            for p in range(left_rows.shape[0]):
                part = lax.dot_general(
                    left_rows[p], right_rows[p], (((1,), (1,)), ((), ())),
                    preferred_element_type=jnp.float32,
                )
                total = part if total is None else total + part
        out_ref[0] = total

    @pl.when(jnp.logical_not(live))
    def _():
        out_ref[...] = jnp.zeros_like(out_ref)


CHUNKS = 2


def on_device(pair_list, pair_count, tiles, coeff):
    pair_slots = pair_list.shape[0]
    aux_local = tiles.shape[1]
    block_size = tiles.shape[2]
    orbitals = coeff.shape[1]
    own_blocks = coeff.shape[0] // block_size
    window_blocks = (BAND + 1) * own_blocks
    width = orbitals // CHUNKS
    devices = lax.axis_size("ao")
    owner_index = lax.axis_index("ao")
    first_block = owner_index * own_blocks
    left_rel = (pair_list[:, 0] - first_block).astype(jnp.int32)
    right_rel = (pair_list[:, 1] - first_block).astype(jnp.int32)
    count = pair_count.astype(jnp.int32)
    own_coeff = coeff.reshape(own_blocks, block_size, orbitals)
    ahead_coeff = [passed_along(own_coeff, "ao", -distance) for distance in range(1, BAND + 1)]
    window_coeff = jnp.concatenate([own_coeff] + ahead_coeff, 0)

    def tile_map(slot, left, right, cnt):
        return (jnp.minimum(slot, jnp.maximum(cnt[0] - 1, 0)), 0, 0, 0)

    halves = pl.pallas_call(
        _half_kernel,
        grid_spec=pltpu.PrefetchScalarGridSpec(
            num_scalar_prefetch=3,
            grid=(pair_slots,),
            in_specs=[
                pl.BlockSpec((1, aux_local, block_size, block_size), tile_map),
                pl.BlockSpec(
                    (window_blocks, block_size, orbitals), lambda s, l, r, c: (0, 0, 0)
                ),
            ],
            out_specs=pl.BlockSpec(
                (CHUNKS, window_blocks, aux_local, block_size, width),
                lambda s, l, r, c: (0, 0, 0, 0, 0),
            ),
            scratch_shapes=[
                pltpu.VMEM((window_blocks, aux_local, block_size, orbitals), jnp.float32)
            ],
        ),
        out_shape=jax.ShapeDtypeStruct(
            (CHUNKS, window_blocks, aux_local, block_size, width), jnp.bfloat16
        ),
        compiler_params=pltpu.CompilerParams(
            dimension_semantics=("arbitrary",), vmem_limit_bytes=48 * 1024 * 1024
        ),
    )(left_rel, right_rel, count, tiles, window_coeff)

    odd_down_one = [(s, s - 1) for s in range(1, devices, 2)]
    odd_down_two = [(s, s - 2) for s in range(3, devices, 2)]
    is_even = (owner_index % 2) == 0
    block_shape = (own_blocks, aux_local, block_size, width)
    pieces = []
    pending = halves[0]
    for c in range(CHUNKS):
        chunk = pending
        from_one = passed_along(chunk[own_blocks : 2 * own_blocks], "ao", 1)
        from_two = passed_along(chunk[2 * own_blocks :], "ao", 2)
        fitted = (
            (from_two.astype(jnp.float32) + from_one.astype(jnp.float32))
            + chunk[:own_blocks].astype(jnp.float32)
        ).astype(jnp.bfloat16)
        if c + 1 < CHUNKS:
            fitted, pending = lax.optimization_barrier((fitted, halves[c + 1]))
        near = passed_along(fitted, "ao", -1)
        relayed = lax.ppermute(near, "ao", odd_down_one)
        direct = lax.ppermute(fitted, "ao", odd_down_two)
        far = jnp.where(is_even, relayed, direct)
        pieces += [fitted, near, far]
    whole = pl.BlockSpec(block_shape, lambda s, l, r, n: (0, 0, 0, 0))
    partial_tiles = pl.pallas_call(
        _contract_kernel,
        grid_spec=pltpu.PrefetchScalarGridSpec(
            num_scalar_prefetch=3,
            grid=(pair_slots,),
            in_specs=[whole] * len(pieces),
            out_specs=pl.BlockSpec((1, block_size, block_size), lambda s, l, r, n: (s, 0, 0)),
        ),
        out_shape=jax.ShapeDtypeStruct((pair_slots, block_size, block_size), jnp.float32),
        compiler_params=pltpu.CompilerParams(
            dimension_semantics=("arbitrary",), vmem_limit_bytes=48 * 1024 * 1024
        ),
    )(left_rel, right_rel, count, *pieces)

    summed = lax.psum_scatter(
        partial_tiles.astype(jnp.bfloat16), "aux", scatter_dimension=1, tiled=True
    )
    norm_factor = (aux_local * lax.axis_size("aux") * orbitals) ** (-0.5)
    return (summed.astype(jnp.float32) * norm_factor).astype(jnp.bfloat16)


def solution(mesh):
    in_specs = (P("ao", None), P("ao"), P("ao", "aux", None, None), P("ao", None))
    out_specs = P("ao", "aux", None)
    return jax.shard_map(
        on_device, mesh=mesh, in_specs=in_specs, out_specs=out_specs, check_vma=False
    )
```

```python
import jax
import jax.numpy as jnp
from jax import lax
from jax.experimental import pallas as pl
from jax.experimental.pallas import tpu as pltpu
from jax.sharding import PartitionSpec as P

BAND = 2


def passed_along(value, axis, steps):
    count = lax.axis_size(axis)
    first, last = (max(0, -steps), min(count, count - steps))
    return lax.ppermute(value, axis, [(source, source + steps) for source in range(first, last)])


def _half_kernel(left_ref, right_ref, count_ref, tile_ref, coeff_ref, out_ref, acc_ref):
    slot = pl.program_id(0)

    @pl.when(slot == 0)
    def _():
        acc_ref[...] = jnp.zeros_like(acc_ref)

    @pl.when(slot < count_ref[0])
    def _():
        left = left_ref[slot]
        right = right_ref[slot]
        tile = tile_ref[0]
        aux_local, block_size, _ = tile.shape
        right_coeff = coeff_ref[right]
        left_coeff = coeff_ref[left]
        to_left = jnp.dot(
            tile.reshape(aux_local * block_size, block_size),
            right_coeff,
            preferred_element_type=jnp.float32,
        ).reshape(aux_local, block_size, -1)
        acc_ref[left] += to_left
        parts = [
            lax.dot_general(
                tile[p], left_coeff, (((0,), (0,)), ((), ())),
                preferred_element_type=jnp.float32,
            )
            for p in range(aux_local)
        ]
        acc_ref[right] += jnp.stack(parts, 0)

    @pl.when(slot == pl.num_programs(0) - 1)
    def _():
        chunks = out_ref.shape[0]
        width = out_ref.shape[-1]
        for c in range(chunks):
            out_ref[c] = acc_ref[:, :, :, c * width : (c + 1) * width].astype(out_ref.dtype)


def _contract_kernel(left_ref, right_ref, count_ref, *refs):
    out_ref = refs[-1]
    groups = refs[:-1]
    chunks = len(groups) // 3
    slot = pl.program_id(0)
    live = slot < count_ref[0]
    own_blocks = groups[0].shape[0]

    @pl.when(live)
    def _():
        left = left_ref[slot]
        right = right_ref[slot]
        group = right // own_blocks
        index = right % own_blocks
        total = None
        for c in range(chunks):
            own_ref, near_ref, far_ref = groups[3 * c : 3 * c + 3]
            left_rows = own_ref[left]
            right_rows = jnp.where(
                group == 0, own_ref[index], jnp.where(group == 1, near_ref[index], far_ref[index])
            )
            for p in range(left_rows.shape[0]):
                part = lax.dot_general(
                    left_rows[p], right_rows[p], (((1,), (1,)), ((), ())),
                    preferred_element_type=jnp.float32,
                )
                total = part if total is None else total + part
        out_ref[:, 0] = total.reshape(out_ref.shape[0], out_ref.shape[2], out_ref.shape[3])

    @pl.when(jnp.logical_not(live))
    def _():
        out_ref[...] = jnp.zeros_like(out_ref)


CHUNKS = 2


def on_device(pair_list, pair_count, tiles, coeff):
    pair_slots = pair_list.shape[0]
    aux_local = tiles.shape[1]
    block_size = tiles.shape[2]
    orbitals = coeff.shape[1]
    own_blocks = coeff.shape[0] // block_size
    window_blocks = (BAND + 1) * own_blocks
    width = orbitals // CHUNKS
    devices = lax.axis_size("ao")
    owner_index = lax.axis_index("ao")
    first_block = owner_index * own_blocks
    left_rel = (pair_list[:, 0] - first_block).astype(jnp.int32)
    right_rel = (pair_list[:, 1] - first_block).astype(jnp.int32)
    count = pair_count.astype(jnp.int32)
    own_coeff = coeff.reshape(own_blocks, block_size, orbitals)
    ahead_coeff = [passed_along(own_coeff, "ao", -distance) for distance in range(1, BAND + 1)]
    window_coeff = jnp.concatenate([own_coeff] + ahead_coeff, 0)

    def tile_map(slot, left, right, cnt):
        return (jnp.minimum(slot, jnp.maximum(cnt[0] - 1, 0)), 0, 0, 0)

    halves = pl.pallas_call(
        _half_kernel,
        grid_spec=pltpu.PrefetchScalarGridSpec(
            num_scalar_prefetch=3,
            grid=(pair_slots,),
            in_specs=[
                pl.BlockSpec((1, aux_local, block_size, block_size), tile_map),
                pl.BlockSpec(
                    (window_blocks, block_size, orbitals), lambda s, l, r, c: (0, 0, 0)
                ),
            ],
            out_specs=pl.BlockSpec(
                (CHUNKS, window_blocks, aux_local, block_size, width),
                lambda s, l, r, c: (0, 0, 0, 0, 0),
            ),
            scratch_shapes=[
                pltpu.VMEM((window_blocks, aux_local, block_size, orbitals), jnp.float32)
            ],
        ),
        out_shape=jax.ShapeDtypeStruct(
            (CHUNKS, window_blocks, aux_local, block_size, width), jnp.bfloat16
        ),
        compiler_params=pltpu.CompilerParams(
            dimension_semantics=("arbitrary",), vmem_limit_bytes=48 * 1024 * 1024
        ),
    )(left_rel, right_rel, count, tiles, window_coeff)

    odd_down_one = [(s, s - 1) for s in range(1, devices, 2)]
    odd_down_two = [(s, s - 2) for s in range(3, devices, 2)]
    is_even = (owner_index % 2) == 0
    block_shape = (own_blocks, aux_local, block_size, width)
    pieces = []
    pending = halves[0]
    for c in range(CHUNKS):
        chunk = pending
        from_one = passed_along(chunk[own_blocks : 2 * own_blocks], "ao", 1)
        from_two = passed_along(chunk[2 * own_blocks :], "ao", 2)
        fitted = (
            (from_two.astype(jnp.float32) + from_one.astype(jnp.float32))
            + chunk[:own_blocks].astype(jnp.float32)
        ).astype(jnp.bfloat16)
        if c + 1 < CHUNKS:
            fitted, pending = lax.optimization_barrier((fitted, halves[c + 1]))
        near = passed_along(fitted, "ao", -1)
        relayed = lax.ppermute(near, "ao", odd_down_one)
        direct = lax.ppermute(fitted, "ao", odd_down_two)
        far = jnp.where(is_even, relayed, direct)
        pieces += [fitted, near, far]
    aux_devices = lax.axis_size("aux")
    share = block_size // aux_devices
    whole = pl.BlockSpec(block_shape, lambda s, l, r, n: (0, 0, 0, 0))
    partial_tiles = pl.pallas_call(
        _contract_kernel,
        grid_spec=pltpu.PrefetchScalarGridSpec(
            num_scalar_prefetch=3,
            grid=(pair_slots,),
            in_specs=[whole] * len(pieces),
            out_specs=pl.BlockSpec(
                (aux_devices, 1, share, block_size), lambda s, l, r, n: (0, s, 0, 0)
            ),
        ),
        out_shape=jax.ShapeDtypeStruct(
            (aux_devices, pair_slots, share, block_size), jnp.float32
        ),
        compiler_params=pltpu.CompilerParams(
            dimension_semantics=("arbitrary",), vmem_limit_bytes=48 * 1024 * 1024
        ),
    )(left_rel, right_rel, count, *pieces)

    gathered = lax.all_to_all(partial_tiles, "aux", 0, 0, tiled=True)
    summed = gathered[0]
    for source in range(1, aux_devices):
        summed = summed + gathered[source]
    norm_factor = (aux_local * lax.axis_size("aux") * orbitals) ** (-0.5)
    return (summed * norm_factor).astype(jnp.bfloat16)


def solution(mesh):
    in_specs = (P("ao", None), P("ao"), P("ao", "aux", None, None), P("ao", None))
    out_specs = P("ao", "aux", None)
    return jax.shard_map(
        on_device, mesh=mesh, in_specs=in_specs, out_specs=out_specs, check_vma=False
    )
```

```python
import jax
import jax.numpy as jnp
from jax import lax
from jax.experimental import pallas as pl
from jax.experimental.pallas import tpu as pltpu
from jax.sharding import PartitionSpec as P

BAND = 2


def passed_along(value, axis, steps):
    count = lax.axis_size(axis)
    first, last = (max(0, -steps), min(count, count - steps))
    return lax.ppermute(value, axis, [(source, source + steps) for source in range(first, last)])


def _half_kernel(left_ref, right_ref, count_ref, tile_ref, coeff_ref, out_ref, acc_ref):
    slot = pl.program_id(0)

    @pl.when(slot == 0)
    def _():
        acc_ref[...] = jnp.zeros_like(acc_ref)

    @pl.when(slot < count_ref[0])
    def _():
        left = left_ref[slot]
        right = right_ref[slot]
        tile = tile_ref[0]
        aux_local, block_size, _ = tile.shape
        right_coeff = coeff_ref[right]
        left_coeff = coeff_ref[left]
        to_left = jnp.dot(
            tile.reshape(aux_local * block_size, block_size),
            right_coeff,
            preferred_element_type=jnp.float32,
        ).reshape(aux_local, block_size, -1)
        acc_ref[left] += to_left
        parts = [
            lax.dot_general(
                tile[p], left_coeff, (((0,), (0,)), ((), ())),
                preferred_element_type=jnp.float32,
            )
            for p in range(aux_local)
        ]
        acc_ref[right] += jnp.stack(parts, 0)

    @pl.when(slot == pl.num_programs(0) - 1)
    def _():
        chunks = out_ref.shape[0]
        width = out_ref.shape[-1]
        for c in range(chunks):
            out_ref[c] = acc_ref[:, :, :, c * width : (c + 1) * width].astype(out_ref.dtype)


def _contract_kernel(left_ref, right_ref, count_ref, *refs):
    out_ref = refs[-1]
    groups = refs[:-1]
    chunks = len(groups) // 3
    slot = pl.program_id(0)
    live = slot < count_ref[0]
    own_blocks = groups[0].shape[0]

    @pl.when(live)
    def _():
        left = left_ref[slot]
        right = right_ref[slot]
        group = right // own_blocks
        index = right % own_blocks
        total = None
        for c in range(chunks):
            own_ref, near_ref, far_ref = groups[3 * c : 3 * c + 3]
            left_rows = own_ref[left]
            right_rows = jnp.where(
                group == 0, own_ref[index], jnp.where(group == 1, near_ref[index], far_ref[index])
            )
            for p in range(left_rows.shape[0]):
                part = lax.dot_general(
                    left_rows[p], right_rows[p], (((1,), (1,)), ((), ())),
                    preferred_element_type=jnp.float32,
                )
                total = part if total is None else total + part
        out_ref[:, 0] = total.reshape(out_ref.shape[0], out_ref.shape[2], out_ref.shape[3])

    @pl.when(jnp.logical_not(live))
    def _():
        out_ref[...] = jnp.zeros_like(out_ref)


CHUNKS = 1


def on_device(pair_list, pair_count, tiles, coeff):
    pair_slots = pair_list.shape[0]
    aux_local = tiles.shape[1]
    block_size = tiles.shape[2]
    orbitals = coeff.shape[1]
    own_blocks = coeff.shape[0] // block_size
    window_blocks = (BAND + 1) * own_blocks
    width = orbitals // CHUNKS
    devices = lax.axis_size("ao")
    owner_index = lax.axis_index("ao")
    first_block = owner_index * own_blocks
    left_rel = (pair_list[:, 0] - first_block).astype(jnp.int32)
    right_rel = (pair_list[:, 1] - first_block).astype(jnp.int32)
    count = pair_count.astype(jnp.int32)
    own_coeff = coeff.reshape(own_blocks, block_size, orbitals)
    ahead_coeff = [passed_along(own_coeff, "ao", -distance) for distance in range(1, BAND + 1)]
    window_coeff = jnp.concatenate([own_coeff] + ahead_coeff, 0)

    def tile_map(slot, left, right, cnt):
        return (jnp.minimum(slot, jnp.maximum(cnt[0] - 1, 0)), 0, 0, 0)

    halves = pl.pallas_call(
        _half_kernel,
        grid_spec=pltpu.PrefetchScalarGridSpec(
            num_scalar_prefetch=3,
            grid=(pair_slots,),
            in_specs=[
                pl.BlockSpec((1, aux_local, block_size, block_size), tile_map),
                pl.BlockSpec(
                    (window_blocks, block_size, orbitals), lambda s, l, r, c: (0, 0, 0)
                ),
            ],
            out_specs=pl.BlockSpec(
                (CHUNKS, window_blocks, aux_local, block_size, width),
                lambda s, l, r, c: (0, 0, 0, 0, 0),
            ),
            scratch_shapes=[
                pltpu.VMEM((window_blocks, aux_local, block_size, orbitals), jnp.float32)
            ],
        ),
        out_shape=jax.ShapeDtypeStruct(
            (CHUNKS, window_blocks, aux_local, block_size, width), jnp.bfloat16
        ),
        compiler_params=pltpu.CompilerParams(
            dimension_semantics=("arbitrary",), vmem_limit_bytes=48 * 1024 * 1024
        ),
    )(left_rel, right_rel, count, tiles, window_coeff)

    odd_down_one = [(s, s - 1) for s in range(1, devices, 2)]
    odd_down_two = [(s, s - 2) for s in range(3, devices, 2)]
    is_even = (owner_index % 2) == 0
    block_shape = (own_blocks, aux_local, block_size, width)
    pieces = []
    pending = halves[0]
    for c in range(CHUNKS):
        chunk = pending
        from_one = passed_along(chunk[own_blocks : 2 * own_blocks], "ao", 1)
        from_two = passed_along(chunk[2 * own_blocks :], "ao", 2)
        fitted = (
            (from_two.astype(jnp.float32) + from_one.astype(jnp.float32))
            + chunk[:own_blocks].astype(jnp.float32)
        ).astype(jnp.bfloat16)
        if c + 1 < CHUNKS:
            fitted, pending = lax.optimization_barrier((fitted, halves[c + 1]))
        near = passed_along(fitted, "ao", -1)
        relayed = lax.ppermute(near, "ao", odd_down_one)
        direct = lax.ppermute(fitted, "ao", odd_down_two)
        far = jnp.where(is_even, relayed, direct)
        pieces += [fitted, near, far]
    aux_devices = lax.axis_size("aux")
    share = block_size // aux_devices
    whole = pl.BlockSpec(block_shape, lambda s, l, r, n: (0, 0, 0, 0))
    partial_tiles = pl.pallas_call(
        _contract_kernel,
        grid_spec=pltpu.PrefetchScalarGridSpec(
            num_scalar_prefetch=3,
            grid=(pair_slots,),
            in_specs=[whole] * len(pieces),
            out_specs=pl.BlockSpec(
                (aux_devices, 1, share, block_size), lambda s, l, r, n: (0, s, 0, 0)
            ),
        ),
        out_shape=jax.ShapeDtypeStruct(
            (aux_devices, pair_slots, share, block_size), jnp.float32
        ),
        compiler_params=pltpu.CompilerParams(
            dimension_semantics=("arbitrary",), vmem_limit_bytes=48 * 1024 * 1024
        ),
    )(left_rel, right_rel, count, *pieces)

    gathered = lax.all_to_all(partial_tiles, "aux", 0, 0, tiled=True)
    summed = gathered[0]
    for source in range(1, aux_devices):
        summed = summed + gathered[source]
    norm_factor = (aux_local * lax.axis_size("aux") * orbitals) ** (-0.5)
    return (summed * norm_factor).astype(jnp.bfloat16)


def solution(mesh):
    in_specs = (P("ao", None), P("ao"), P("ao", "aux", None, None), P("ao", None))
    out_specs = P("ao", "aux", None)
    return jax.shard_map(
        on_device, mesh=mesh, in_specs=in_specs, out_specs=out_specs, check_vma=False
    )
```

```python
import jax
import jax.numpy as jnp
from jax import lax
from jax.experimental import pallas as pl
from jax.experimental.pallas import tpu as pltpu
from jax.sharding import PartitionSpec as P

BAND = 2


def passed_along(value, axis, steps):
    count = lax.axis_size(axis)
    first, last = (max(0, -steps), min(count, count - steps))
    return lax.ppermute(value, axis, [(source, source + steps) for source in range(first, last)])


def _half_kernel(left_ref, right_ref, count_ref, tile_ref, coeff_ref, out_ref, acc_ref):
    slot = pl.program_id(0)

    @pl.when(slot == 0)
    def _():
        acc_ref[...] = jnp.zeros_like(acc_ref)

    @pl.when(slot < count_ref[0])
    def _():
        left = left_ref[slot]
        right = right_ref[slot]
        tile = tile_ref[0]
        aux_local, block_size, _ = tile.shape
        right_coeff = coeff_ref[right]
        left_coeff = coeff_ref[left]
        to_left = jnp.dot(
            tile.reshape(aux_local * block_size, block_size),
            right_coeff,
            preferred_element_type=jnp.float32,
        ).reshape(aux_local, block_size, -1)
        acc_ref[left] += to_left
        parts = [
            lax.dot_general(
                tile[p], left_coeff, (((0,), (0,)), ((), ())),
                preferred_element_type=jnp.float32,
            )
            for p in range(aux_local)
        ]
        acc_ref[right] += jnp.stack(parts, 0)

    @pl.when(slot == pl.num_programs(0) - 1)
    def _():
        chunks = out_ref.shape[0]
        width = out_ref.shape[-1]
        for c in range(chunks):
            out_ref[c] = acc_ref[:, :, :, c * width : (c + 1) * width].astype(out_ref.dtype)


def _contract_kernel(left_ref, right_ref, count_ref, *refs):
    out_ref = refs[-1]
    groups = refs[:-1]
    chunks = len(groups) // 3
    slot = pl.program_id(0)
    live = slot < count_ref[0]
    own_blocks = groups[0].shape[0]

    @pl.when(live)
    def _():
        left = left_ref[slot]
        right = right_ref[slot]
        group = right // own_blocks
        index = right % own_blocks
        total = None
        for c in range(chunks):
            own_ref, near_ref, far_ref = groups[3 * c : 3 * c + 3]
            left_rows = own_ref[left]
            right_rows = jnp.where(
                group == 0, own_ref[index], jnp.where(group == 1, near_ref[index], far_ref[index])
            )
            for p in range(left_rows.shape[0]):
                part = lax.dot_general(
                    left_rows[p], right_rows[p], (((1,), (1,)), ((), ())),
                    preferred_element_type=jnp.float32,
                )
                total = part if total is None else total + part
        out_ref[:, 0] = total.reshape(out_ref.shape[0], out_ref.shape[2], out_ref.shape[3])

    @pl.when(jnp.logical_not(live))
    def _():
        out_ref[...] = jnp.zeros_like(out_ref)


CHUNKS = 1


def on_device(pair_list, pair_count, tiles, coeff):
    pair_slots = pair_list.shape[0]
    aux_local = tiles.shape[1]
    block_size = tiles.shape[2]
    orbitals = coeff.shape[1]
    own_blocks = coeff.shape[0] // block_size
    window_blocks = (BAND + 1) * own_blocks
    width = orbitals // CHUNKS
    devices = lax.axis_size("ao")
    owner_index = lax.axis_index("ao")
    first_block = owner_index * own_blocks
    left_rel = (pair_list[:, 0] - first_block).astype(jnp.int32)
    right_rel = (pair_list[:, 1] - first_block).astype(jnp.int32)
    count = pair_count.astype(jnp.int32)
    own_coeff = coeff.reshape(own_blocks, block_size, orbitals)
    ahead_coeff = [passed_along(own_coeff, "ao", -distance) for distance in range(1, BAND + 1)]
    window_coeff = jnp.concatenate([own_coeff] + ahead_coeff, 0)

    def tile_map(slot, left, right, cnt):
        return (jnp.minimum(slot, jnp.maximum(cnt[0] - 1, 0)), 0, 0, 0)

    halves = pl.pallas_call(
        _half_kernel,
        grid_spec=pltpu.PrefetchScalarGridSpec(
            num_scalar_prefetch=3,
            grid=(pair_slots,),
            in_specs=[
                pl.BlockSpec((1, aux_local, block_size, block_size), tile_map),
                pl.BlockSpec(
                    (window_blocks, block_size, orbitals), lambda s, l, r, c: (0, 0, 0)
                ),
            ],
            out_specs=pl.BlockSpec(
                (CHUNKS, window_blocks, aux_local, block_size, width),
                lambda s, l, r, c: (0, 0, 0, 0, 0),
            ),
            scratch_shapes=[
                pltpu.VMEM((window_blocks, aux_local, block_size, orbitals), jnp.float32)
            ],
        ),
        out_shape=jax.ShapeDtypeStruct(
            (CHUNKS, window_blocks, aux_local, block_size, width), jnp.bfloat16
        ),
        compiler_params=pltpu.CompilerParams(
            dimension_semantics=("arbitrary",), vmem_limit_bytes=48 * 1024 * 1024
        ),
    )(left_rel, right_rel, count, tiles, window_coeff)

    block_shape = (own_blocks, aux_local, block_size, width)
    pieces = []
    for c in range(CHUNKS):
        chunk = halves[c]
        behind_two = passed_along(chunk[2 * own_blocks :], "ao", 2)
        behind_one = passed_along(chunk[own_blocks:], "ao", 1)
        ahead_one = passed_along(chunk[: 2 * own_blocks], "ao", -1)
        ahead_two = passed_along(chunk[:own_blocks], "ao", -2)

        def owner_sum(first, second, third):
            total = first.astype(jnp.float32) + second.astype(jnp.float32)
            return (total + third.astype(jnp.float32)).astype(jnp.bfloat16)

        pieces += [
            owner_sum(behind_two, behind_one[:own_blocks], chunk[:own_blocks]),
            owner_sum(
                behind_one[own_blocks:], chunk[own_blocks : 2 * own_blocks], ahead_one[:own_blocks]
            ),
            owner_sum(chunk[2 * own_blocks :], ahead_one[own_blocks:], ahead_two),
        ]
    aux_devices = lax.axis_size("aux")
    share = block_size // aux_devices
    whole = pl.BlockSpec(block_shape, lambda s, l, r, n: (0, 0, 0, 0))
    partial_tiles = pl.pallas_call(
        _contract_kernel,
        grid_spec=pltpu.PrefetchScalarGridSpec(
            num_scalar_prefetch=3,
            grid=(pair_slots,),
            in_specs=[whole] * len(pieces),
            out_specs=pl.BlockSpec(
                (aux_devices, 1, share, block_size), lambda s, l, r, n: (0, s, 0, 0)
            ),
        ),
        out_shape=jax.ShapeDtypeStruct(
            (aux_devices, pair_slots, share, block_size), jnp.float32
        ),
        compiler_params=pltpu.CompilerParams(
            dimension_semantics=("arbitrary",), vmem_limit_bytes=48 * 1024 * 1024
        ),
    )(left_rel, right_rel, count, *pieces)

    gathered = lax.all_to_all(partial_tiles, "aux", 0, 0, tiled=True)
    summed = gathered[0]
    for source in range(1, aux_devices):
        summed = summed + gathered[source]
    norm_factor = (aux_local * lax.axis_size("aux") * orbitals) ** (-0.5)
    return (summed * norm_factor).astype(jnp.bfloat16)


def solution(mesh):
    in_specs = (P("ao", None), P("ao"), P("ao", "aux", None, None), P("ao", None))
    out_specs = P("ao", "aux", None)
    return jax.shard_map(
        on_device, mesh=mesh, in_specs=in_specs, out_specs=out_specs, check_vma=False
    )
```

```python
import jax
import jax.numpy as jnp
from jax import lax
from jax.experimental import pallas as pl
from jax.experimental.pallas import tpu as pltpu
from jax.sharding import PartitionSpec as P

BAND = 2


def passed_along(value, axis, steps):
    count = lax.axis_size(axis)
    first, last = (max(0, -steps), min(count, count - steps))
    return lax.ppermute(value, axis, [(source, source + steps) for source in range(first, last)])


def _half_kernel(left_ref, right_ref, count_ref, tile_ref, coeff_ref, out_ref, acc_ref):
    slot = pl.program_id(0)

    @pl.when(slot == 0)
    def _():
        acc_ref[...] = jnp.zeros_like(acc_ref)

    @pl.when(slot < count_ref[0])
    def _():
        left = left_ref[slot]
        right = right_ref[slot]
        tile = tile_ref[0]
        aux_local, block_size, _ = tile.shape
        right_coeff = coeff_ref[right]
        left_coeff = coeff_ref[left]
        to_left = jnp.dot(
            tile.reshape(aux_local * block_size, block_size),
            right_coeff,
            preferred_element_type=jnp.float32,
        ).reshape(aux_local, block_size, -1)
        acc_ref[left] += to_left
        parts = [
            lax.dot_general(
                tile[p], left_coeff, (((0,), (0,)), ((), ())),
                preferred_element_type=jnp.float32,
            )
            for p in range(aux_local)
        ]
        acc_ref[right] += jnp.stack(parts, 0)

    @pl.when(slot == pl.num_programs(0) - 1)
    def _():
        chunks = out_ref.shape[0]
        width = out_ref.shape[-1]
        for c in range(chunks):
            out_ref[c] = acc_ref[:, :, :, c * width : (c + 1) * width].astype(out_ref.dtype)


def _contract_kernel(left_ref, right_ref, count_ref, *refs):
    out_ref = refs[-1]
    groups = refs[:-1]
    chunks = len(groups) // 3
    slot = pl.program_id(0)
    live = slot < count_ref[0]
    own_blocks = groups[0].shape[0]

    @pl.when(live)
    def _():
        left = left_ref[slot]
        right = right_ref[slot]
        group = right // own_blocks
        index = right % own_blocks
        total = None
        for c in range(chunks):
            own_ref, near_ref, far_ref = groups[3 * c : 3 * c + 3]
            left_rows = own_ref[left]
            right_rows = jnp.where(
                group == 0, own_ref[index], jnp.where(group == 1, near_ref[index], far_ref[index])
            )
            for p in range(left_rows.shape[0]):
                part = lax.dot_general(
                    left_rows[p], right_rows[p], (((1,), (1,)), ((), ())),
                    preferred_element_type=jnp.float32,
                )
                total = part if total is None else total + part
        out_ref[:, 0] = total.reshape(
            out_ref.shape[0], out_ref.shape[2], out_ref.shape[3]
        ).astype(out_ref.dtype)

    @pl.when(jnp.logical_not(live))
    def _():
        out_ref[...] = jnp.zeros_like(out_ref)


CHUNKS = 1


def on_device(pair_list, pair_count, tiles, coeff):
    pair_slots = pair_list.shape[0]
    aux_local = tiles.shape[1]
    block_size = tiles.shape[2]
    orbitals = coeff.shape[1]
    own_blocks = coeff.shape[0] // block_size
    window_blocks = (BAND + 1) * own_blocks
    width = orbitals // CHUNKS
    devices = lax.axis_size("ao")
    owner_index = lax.axis_index("ao")
    first_block = owner_index * own_blocks
    left_rel = (pair_list[:, 0] - first_block).astype(jnp.int32)
    right_rel = (pair_list[:, 1] - first_block).astype(jnp.int32)
    count = pair_count.astype(jnp.int32)
    own_coeff = coeff.reshape(own_blocks, block_size, orbitals)
    ahead_coeff = [passed_along(own_coeff, "ao", -distance) for distance in range(1, BAND + 1)]
    window_coeff = jnp.concatenate([own_coeff] + ahead_coeff, 0)

    def tile_map(slot, left, right, cnt):
        return (jnp.minimum(slot, jnp.maximum(cnt[0] - 1, 0)), 0, 0, 0)

    halves = pl.pallas_call(
        _half_kernel,
        grid_spec=pltpu.PrefetchScalarGridSpec(
            num_scalar_prefetch=3,
            grid=(pair_slots,),
            in_specs=[
                pl.BlockSpec((1, aux_local, block_size, block_size), tile_map),
                pl.BlockSpec(
                    (window_blocks, block_size, orbitals), lambda s, l, r, c: (0, 0, 0)
                ),
            ],
            out_specs=pl.BlockSpec(
                (CHUNKS, window_blocks, aux_local, block_size, width),
                lambda s, l, r, c: (0, 0, 0, 0, 0),
            ),
            scratch_shapes=[
                pltpu.VMEM((window_blocks, aux_local, block_size, orbitals), jnp.float32)
            ],
        ),
        out_shape=jax.ShapeDtypeStruct(
            (CHUNKS, window_blocks, aux_local, block_size, width), jnp.bfloat16
        ),
        compiler_params=pltpu.CompilerParams(
            dimension_semantics=("arbitrary",), vmem_limit_bytes=48 * 1024 * 1024
        ),
    )(left_rel, right_rel, count, tiles, window_coeff)

    block_shape = (own_blocks, aux_local, block_size, width)
    pieces = []
    for c in range(CHUNKS):
        chunk = halves[c]
        behind_two = passed_along(chunk[2 * own_blocks :], "ao", 2)
        behind_one = passed_along(chunk[own_blocks:], "ao", 1)
        ahead_one = passed_along(chunk[: 2 * own_blocks], "ao", -1)
        ahead_two = passed_along(chunk[:own_blocks], "ao", -2)

        def owner_sum(first, second, third):
            total = first.astype(jnp.float32) + second.astype(jnp.float32)
            return (total + third.astype(jnp.float32)).astype(jnp.bfloat16)

        pieces += [
            owner_sum(behind_two, behind_one[:own_blocks], chunk[:own_blocks]),
            owner_sum(
                behind_one[own_blocks:], chunk[own_blocks : 2 * own_blocks], ahead_one[:own_blocks]
            ),
            owner_sum(chunk[2 * own_blocks :], ahead_one[own_blocks:], ahead_two),
        ]
    aux_devices = lax.axis_size("aux")
    share = block_size // aux_devices
    whole = pl.BlockSpec(block_shape, lambda s, l, r, n: (0, 0, 0, 0))
    partial_tiles = pl.pallas_call(
        _contract_kernel,
        grid_spec=pltpu.PrefetchScalarGridSpec(
            num_scalar_prefetch=3,
            grid=(pair_slots,),
            in_specs=[whole] * len(pieces),
            out_specs=pl.BlockSpec(
                (aux_devices, 1, share, block_size), lambda s, l, r, n: (0, s, 0, 0)
            ),
        ),
        out_shape=jax.ShapeDtypeStruct(
            (aux_devices, pair_slots, share, block_size), jnp.bfloat16
        ),
        compiler_params=pltpu.CompilerParams(
            dimension_semantics=("arbitrary",), vmem_limit_bytes=48 * 1024 * 1024
        ),
    )(left_rel, right_rel, count, *pieces)

    gathered = lax.all_to_all(partial_tiles, "aux", 0, 0, tiled=True)
    summed = gathered[0].astype(jnp.float32)
    for source in range(1, aux_devices):
        summed = summed + gathered[source].astype(jnp.float32)
    norm_factor = (aux_local * lax.axis_size("aux") * orbitals) ** (-0.5)
    return (summed * norm_factor).astype(jnp.bfloat16)


def solution(mesh):
    in_specs = (P("ao", None), P("ao"), P("ao", "aux", None, None), P("ao", None))
    out_specs = P("ao", "aux", None)
    return jax.shard_map(
        on_device, mesh=mesh, in_specs=in_specs, out_specs=out_specs, check_vma=False
    )
```

```python
import jax
import jax.numpy as jnp
from jax import lax
from jax.experimental import pallas as pl
from jax.experimental.pallas import tpu as pltpu
from jax.sharding import PartitionSpec as P

BAND = 2


def passed_along(value, axis, steps):
    count = lax.axis_size(axis)
    first, last = (max(0, -steps), min(count, count - steps))
    return lax.ppermute(value, axis, [(source, source + steps) for source in range(first, last)])


def _half_kernel(left_ref, right_ref, count_ref, tile_ref, coeff_ref, out_ref, acc_ref):
    slot = pl.program_id(0)

    @pl.when(slot == 0)
    def _():
        acc_ref[...] = jnp.zeros_like(acc_ref)

    @pl.when(slot < count_ref[0])
    def _():
        left = left_ref[slot]
        right = right_ref[slot]
        tile = tile_ref[0]
        aux_local, block_size, _ = tile.shape
        right_coeff = coeff_ref[right]
        left_coeff = coeff_ref[left]
        to_left = jnp.dot(
            tile.reshape(aux_local * block_size, block_size),
            right_coeff,
            preferred_element_type=jnp.float32,
        ).reshape(aux_local, block_size, -1)
        acc_ref[left] += to_left
        parts = [
            lax.dot_general(
                tile[p], left_coeff, (((0,), (0,)), ((), ())),
                preferred_element_type=jnp.float32,
            )
            for p in range(aux_local)
        ]
        acc_ref[right] += jnp.stack(parts, 0)

    @pl.when(slot == pl.num_programs(0) - 1)
    def _():
        chunks = out_ref.shape[0]
        width = out_ref.shape[-1]
        for c in range(chunks):
            out_ref[c] = acc_ref[:, :, :, c * width : (c + 1) * width].astype(out_ref.dtype)


def _contract_kernel(left_ref, right_ref, count_ref, *refs):
    out_ref = refs[-1]
    groups = refs[:-1]
    chunks = len(groups) // 3
    slot = pl.program_id(0)
    live = slot < count_ref[0]
    own_blocks = groups[0].shape[0]

    @pl.when(live)
    def _():
        left = left_ref[slot]
        right = right_ref[slot]
        group = right // own_blocks
        index = right % own_blocks
        total = None
        for c in range(chunks):
            own_ref, near_ref, far_ref = groups[3 * c : 3 * c + 3]
            left_rows = own_ref[left]
            right_rows = jnp.where(
                group == 0, own_ref[index], jnp.where(group == 1, near_ref[index], far_ref[index])
            )
            for p in range(left_rows.shape[0]):
                part = lax.dot_general(
                    left_rows[p], right_rows[p], (((1,), (1,)), ((), ())),
                    preferred_element_type=jnp.float32,
                )
                total = part if total is None else total + part
        out_ref[:, 0] = total.reshape(
            out_ref.shape[0], out_ref.shape[2], out_ref.shape[3]
        ).astype(out_ref.dtype)

    @pl.when(jnp.logical_not(live))
    def _():
        out_ref[...] = jnp.zeros_like(out_ref)


CHUNKS = 1


def on_device(pair_list, pair_count, tiles, coeff):
    pair_slots = pair_list.shape[0]
    aux_local = tiles.shape[1]
    block_size = tiles.shape[2]
    orbitals = coeff.shape[1]
    own_blocks = coeff.shape[0] // block_size
    window_blocks = (BAND + 1) * own_blocks
    width = orbitals // CHUNKS
    devices = lax.axis_size("ao")
    owner_index = lax.axis_index("ao")
    first_block = owner_index * own_blocks
    left_rel = (pair_list[:, 0] - first_block).astype(jnp.int32)
    right_rel = (pair_list[:, 1] - first_block).astype(jnp.int32)
    count = pair_count.astype(jnp.int32)
    own_coeff = coeff.reshape(own_blocks, block_size, orbitals)
    ahead_coeff = [passed_along(own_coeff, "ao", -distance) for distance in range(1, BAND + 1)]
    window_coeff = jnp.concatenate([own_coeff] + ahead_coeff, 0)

    def tile_map(slot, left, right, cnt):
        return (jnp.minimum(slot, jnp.maximum(cnt[0] - 1, 0)), 0, 0, 0)

    halves = pl.pallas_call(
        _half_kernel,
        grid_spec=pltpu.PrefetchScalarGridSpec(
            num_scalar_prefetch=3,
            grid=(pair_slots,),
            in_specs=[
                pl.BlockSpec((1, aux_local, block_size, block_size), tile_map),
                pl.BlockSpec(
                    (window_blocks, block_size, orbitals), lambda s, l, r, c: (0, 0, 0)
                ),
            ],
            out_specs=pl.BlockSpec(
                (CHUNKS, window_blocks, aux_local, block_size, width),
                lambda s, l, r, c: (0, 0, 0, 0, 0),
            ),
            scratch_shapes=[
                pltpu.VMEM((window_blocks, aux_local, block_size, orbitals), jnp.float32)
            ],
        ),
        out_shape=jax.ShapeDtypeStruct(
            (CHUNKS, window_blocks, aux_local, block_size, width), jnp.bfloat16
        ),
        compiler_params=pltpu.CompilerParams(
            dimension_semantics=("arbitrary",), vmem_limit_bytes=48 * 1024 * 1024
        ),
    )(left_rel, right_rel, count, tiles, window_coeff)

    block_shape = (own_blocks, aux_local, block_size, width)
    is_even = (owner_index % 2) == 0
    even_up_two = [(s, s + 2) for s in range(0, devices - 2, 2)]
    odd_down_two = [(s, s - 2) for s in range(3, devices, 2)]
    even_up_one = [(s, s + 1) for s in range(0, devices - 1, 2)]
    odd_down_one = [(s, s - 1) for s in range(1, devices, 2)]
    pieces = []
    for c in range(CHUNKS):
        chunk = halves[c]
        behind_one = passed_along(chunk[own_blocks:], "ao", 1)
        ahead_one = passed_along(chunk[: 2 * own_blocks], "ao", -1)
        even_two = lax.ppermute(chunk[2 * own_blocks :], "ao", even_up_two)
        odd_two = lax.ppermute(chunk[:own_blocks], "ao", odd_down_two)
        relay_behind = lax.ppermute(behind_one[own_blocks:], "ao", even_up_one)
        relay_ahead = lax.ppermute(ahead_one[:own_blocks], "ao", odd_down_one)
        behind_two = jnp.where(is_even, even_two, relay_behind)
        ahead_two = jnp.where(is_even, relay_ahead, odd_two)

        def owner_sum(first, second, third):
            total = first.astype(jnp.float32) + second.astype(jnp.float32)
            return (total + third.astype(jnp.float32)).astype(jnp.bfloat16)

        pieces += [
            owner_sum(behind_two, behind_one[:own_blocks], chunk[:own_blocks]),
            owner_sum(
                behind_one[own_blocks:], chunk[own_blocks : 2 * own_blocks], ahead_one[:own_blocks]
            ),
            owner_sum(chunk[2 * own_blocks :], ahead_one[own_blocks:], ahead_two),
        ]
    aux_devices = lax.axis_size("aux")
    share = block_size // aux_devices
    whole = pl.BlockSpec(block_shape, lambda s, l, r, n: (0, 0, 0, 0))
    partial_tiles = pl.pallas_call(
        _contract_kernel,
        grid_spec=pltpu.PrefetchScalarGridSpec(
            num_scalar_prefetch=3,
            grid=(pair_slots,),
            in_specs=[whole] * len(pieces),
            out_specs=pl.BlockSpec(
                (aux_devices, 1, share, block_size), lambda s, l, r, n: (0, s, 0, 0)
            ),
        ),
        out_shape=jax.ShapeDtypeStruct(
            (aux_devices, pair_slots, share, block_size), jnp.bfloat16
        ),
        compiler_params=pltpu.CompilerParams(
            dimension_semantics=("arbitrary",), vmem_limit_bytes=48 * 1024 * 1024
        ),
    )(left_rel, right_rel, count, *pieces)

    gathered = lax.all_to_all(partial_tiles, "aux", 0, 0, tiled=True)
    summed = gathered[0].astype(jnp.float32)
    for source in range(1, aux_devices):
        summed = summed + gathered[source].astype(jnp.float32)
    norm_factor = (aux_local * lax.axis_size("aux") * orbitals) ** (-0.5)
    return (summed * norm_factor).astype(jnp.bfloat16)


def solution(mesh):
    in_specs = (P("ao", None), P("ao"), P("ao", "aux", None, None), P("ao", None))
    out_specs = P("ao", "aux", None)
    return jax.shard_map(
        on_device, mesh=mesh, in_specs=in_specs, out_specs=out_specs, check_vma=False
    )
```

```python
import jax
import jax.numpy as jnp
from jax import lax
from jax.experimental import pallas as pl
from jax.experimental.pallas import tpu as pltpu
from jax.sharding import PartitionSpec as P

BAND = 2


def passed_along(value, axis, steps):
    count = lax.axis_size(axis)
    first, last = (max(0, -steps), min(count, count - steps))
    return lax.ppermute(value, axis, [(source, source + steps) for source in range(first, last)])


def _right_kernel(left_ref, right_ref, count_ref, tile_ref, coeff_ref, hi_ref, part_ref, acc_ref):
    slot = pl.program_id(0)
    own_blocks = part_ref.shape[0]

    @pl.when(slot == 0)
    def _():
        acc_ref[...] = jnp.zeros_like(acc_ref)

    @pl.when(slot < count_ref[0])
    def _():
        tile = tile_ref[0]
        left_coeff = coeff_ref[left_ref[slot]]
        parts = [
            lax.dot_general(
                tile[p], left_coeff, (((0,), (0,)), ((), ())),
                preferred_element_type=jnp.float32,
            )
            for p in range(tile.shape[0])
        ]
        right = right_ref[slot]
        acc_ref[right] += jnp.stack(parts, 0)

    @pl.when(slot == pl.num_programs(0) - 1)
    def _():
        part_ref[...] = acc_ref[:own_blocks]
        hi_ref[...] = acc_ref[own_blocks:].astype(hi_ref.dtype)


def _left_kernel(left_ref, right_ref, count_ref, tile_ref, coeff_ref, part_ref, hi_ref, lo_ref, acc_ref):
    slot = pl.program_id(0)
    own_blocks = part_ref.shape[0]

    @pl.when(slot == 0)
    def _():
        acc_ref[...] = part_ref[...]

    @pl.when(slot < count_ref[0])
    def _():
        tile = tile_ref[0]
        aux_local, block_size, _ = tile.shape
        to_left = jnp.dot(
            tile.reshape(aux_local * block_size, block_size),
            coeff_ref[right_ref[slot]],
            preferred_element_type=jnp.float32,
        ).reshape(aux_local, block_size, -1)
        left = left_ref[slot]
        acc_ref[left] += to_left

    @pl.when(slot == pl.num_programs(0) - 1)
    def _():
        lo_ref[:own_blocks] = acc_ref[...].astype(lo_ref.dtype)
        lo_ref[own_blocks:] = hi_ref[:own_blocks]


def _contract_kernel(left_ref, right_ref, count_ref, *refs):
    out_ref = refs[-1]
    groups = refs[:-1]
    chunks = len(groups) // 3
    slot = pl.program_id(0)
    live = slot < count_ref[0]
    own_blocks = groups[0].shape[0]

    @pl.when(live)
    def _():
        left = left_ref[slot]
        right = right_ref[slot]
        group = right // own_blocks
        index = right % own_blocks
        total = None
        for c in range(chunks):
            own_ref, near_ref, far_ref = groups[3 * c : 3 * c + 3]
            left_rows = own_ref[left]
            right_rows = jnp.where(
                group == 0, own_ref[index], jnp.where(group == 1, near_ref[index], far_ref[index])
            )
            for p in range(left_rows.shape[0]):
                part = lax.dot_general(
                    left_rows[p], right_rows[p], (((1,), (1,)), ((), ())),
                    preferred_element_type=jnp.float32,
                )
                total = part if total is None else total + part
        out_ref[:, 0] = total.reshape(
            out_ref.shape[0], out_ref.shape[2], out_ref.shape[3]
        ).astype(out_ref.dtype)

    @pl.when(jnp.logical_not(live))
    def _():
        out_ref[...] = jnp.zeros_like(out_ref)


CHUNKS = 1


def on_device(pair_list, pair_count, tiles, coeff):
    pair_slots = pair_list.shape[0]
    aux_local = tiles.shape[1]
    block_size = tiles.shape[2]
    orbitals = coeff.shape[1]
    own_blocks = coeff.shape[0] // block_size
    window_blocks = (BAND + 1) * own_blocks
    width = orbitals // CHUNKS
    devices = lax.axis_size("ao")
    owner_index = lax.axis_index("ao")
    first_block = owner_index * own_blocks
    left_rel = (pair_list[:, 0] - first_block).astype(jnp.int32)
    right_rel = (pair_list[:, 1] - first_block).astype(jnp.int32)
    count = pair_count.astype(jnp.int32)
    own_coeff = coeff.reshape(own_blocks, block_size, orbitals)
    ahead_coeff = [passed_along(own_coeff, "ao", -distance) for distance in range(1, BAND + 1)]

    def tile_map(slot, left, right, cnt):
        return (jnp.minimum(slot, jnp.maximum(cnt[0] - 1, 0)), 0, 0, 0)

    def fixed(shape):
        return pl.BlockSpec(shape, lambda s, l, r, c: (0,) * len(shape))

    tile_spec = pl.BlockSpec((1, aux_local, block_size, block_size), tile_map)
    own_shape = (own_blocks, aux_local, block_size, orbitals)
    wide_shape = (2 * own_blocks, aux_local, block_size, orbitals)
    params = pltpu.CompilerParams(
        dimension_semantics=("arbitrary",), vmem_limit_bytes=48 * 1024 * 1024
    )
    hi, part = pl.pallas_call(
        _right_kernel,
        grid_spec=pltpu.PrefetchScalarGridSpec(
            num_scalar_prefetch=3,
            grid=(pair_slots,),
            in_specs=[tile_spec, fixed((own_blocks, block_size, orbitals))],
            out_specs=[fixed(wide_shape), fixed(own_shape)],
            scratch_shapes=[pltpu.VMEM((window_blocks,) + own_shape[1:], jnp.float32)],
        ),
        out_shape=[
            jax.ShapeDtypeStruct(wide_shape, jnp.bfloat16),
            jax.ShapeDtypeStruct(own_shape, jnp.float32),
        ],
        compiler_params=params,
    )(left_rel, right_rel, count, tiles, own_coeff)
    window_coeff = jnp.concatenate([own_coeff] + ahead_coeff, 0)
    lo = pl.pallas_call(
        _left_kernel,
        grid_spec=pltpu.PrefetchScalarGridSpec(
            num_scalar_prefetch=3,
            grid=(pair_slots,),
            in_specs=[
                tile_spec,
                fixed((window_blocks, block_size, orbitals)),
                fixed(own_shape),
                fixed(wide_shape),
            ],
            out_specs=fixed(wide_shape),
            scratch_shapes=[pltpu.VMEM(own_shape, jnp.float32)],
        ),
        out_shape=jax.ShapeDtypeStruct(wide_shape, jnp.bfloat16),
        compiler_params=params,
    )(left_rel, right_rel, count, tiles, window_coeff, part, hi)

    block_shape = own_shape
    is_even = (owner_index % 2) == 0
    even_up_two = [(s, s + 2) for s in range(0, devices - 2, 2)]
    odd_down_two = [(s, s - 2) for s in range(3, devices, 2)]
    even_up_one = [(s, s + 1) for s in range(0, devices - 1, 2)]
    odd_down_one = [(s, s - 1) for s in range(1, devices, 2)]
    pieces = []
    for c in range(1):
        behind_one = passed_along(hi, "ao", 1)
        even_two = lax.ppermute(hi[own_blocks:], "ao", even_up_two)
        ahead_one = passed_along(lo, "ao", -1)
        odd_two = lax.ppermute(lo[:own_blocks], "ao", odd_down_two)
        relay_behind = lax.ppermute(behind_one[own_blocks:], "ao", even_up_one)
        relay_ahead = lax.ppermute(ahead_one[:own_blocks], "ao", odd_down_one)
        behind_two = jnp.where(is_even, even_two, relay_behind)
        ahead_two = jnp.where(is_even, relay_ahead, odd_two)

        def owner_sum(first, second, third):
            total = first.astype(jnp.float32) + second.astype(jnp.float32)
            return (total + third.astype(jnp.float32)).astype(jnp.bfloat16)

        pieces += [
            owner_sum(behind_two, behind_one[:own_blocks], lo[:own_blocks]),
            owner_sum(
                behind_one[own_blocks:], hi[:own_blocks], ahead_one[:own_blocks]
            ),
            owner_sum(hi[own_blocks:], ahead_one[own_blocks:], ahead_two),
        ]
    aux_devices = lax.axis_size("aux")
    share = block_size // aux_devices
    whole = pl.BlockSpec(block_shape, lambda s, l, r, n: (0, 0, 0, 0))
    partial_tiles = pl.pallas_call(
        _contract_kernel,
        grid_spec=pltpu.PrefetchScalarGridSpec(
            num_scalar_prefetch=3,
            grid=(pair_slots,),
            in_specs=[whole] * len(pieces),
            out_specs=pl.BlockSpec(
                (aux_devices, 1, share, block_size), lambda s, l, r, n: (0, s, 0, 0)
            ),
        ),
        out_shape=jax.ShapeDtypeStruct(
            (aux_devices, pair_slots, share, block_size), jnp.bfloat16
        ),
        compiler_params=pltpu.CompilerParams(
            dimension_semantics=("arbitrary",), vmem_limit_bytes=48 * 1024 * 1024
        ),
    )(left_rel, right_rel, count, *pieces)

    gathered = lax.all_to_all(partial_tiles, "aux", 0, 0, tiled=True)
    summed = gathered[0].astype(jnp.float32)
    for source in range(1, aux_devices):
        summed = summed + gathered[source].astype(jnp.float32)
    norm_factor = (aux_local * lax.axis_size("aux") * orbitals) ** (-0.5)
    return (summed * norm_factor).astype(jnp.bfloat16)


def solution(mesh):
    in_specs = (P("ao", None), P("ao"), P("ao", "aux", None, None), P("ao", None))
    out_specs = P("ao", "aux", None)
    return jax.shard_map(
        on_device, mesh=mesh, in_specs=in_specs, out_specs=out_specs, check_vma=False
    )
```

```python
import jax
import jax.numpy as jnp
from jax import lax
from jax.experimental import pallas as pl
from jax.experimental.pallas import tpu as pltpu
from jax.sharding import PartitionSpec as P

BAND = 2


def passed_along(value, axis, steps):
    count = lax.axis_size(axis)
    first, last = (max(0, -steps), min(count, count - steps))
    return lax.ppermute(value, axis, [(source, source + steps) for source in range(first, last)])


def _right_kernel(left_ref, right_ref, count_ref, tile_ref, coeff_ref, hi_ref, part_ref, acc_ref):
    slot = pl.program_id(0)
    own_blocks = part_ref.shape[0]

    @pl.when(slot == 0)
    def _():
        acc_ref[...] = jnp.zeros_like(acc_ref)

    @pl.when(slot < count_ref[0])
    def _():
        tile = tile_ref[0]
        left_coeff = coeff_ref[left_ref[slot]]
        parts = [
            lax.dot_general(
                tile[p], left_coeff, (((0,), (0,)), ((), ())),
                preferred_element_type=jnp.float32,
            )
            for p in range(tile.shape[0])
        ]
        right = right_ref[slot]
        acc_ref[right] += jnp.stack(parts, 0)

    @pl.when(slot == pl.num_programs(0) - 1)
    def _():
        part_ref[...] = acc_ref[:own_blocks]
        hi_ref[...] = acc_ref[own_blocks:].astype(hi_ref.dtype)


def _left_kernel(left_ref, right_ref, count_ref, tile_ref, coeff_ref, part_ref, hi_ref, lo_ref, acc_ref):
    slot = pl.program_id(0)
    own_blocks = part_ref.shape[0]

    @pl.when(slot == 0)
    def _():
        acc_ref[...] = part_ref[...]

    @pl.when(slot < count_ref[0])
    def _():
        tile = tile_ref[0]
        aux_local, block_size, _ = tile.shape
        to_left = jnp.dot(
            tile.reshape(aux_local * block_size, block_size),
            coeff_ref[right_ref[slot]],
            preferred_element_type=jnp.float32,
        ).reshape(aux_local, block_size, -1)
        left = left_ref[slot]
        acc_ref[left] += to_left

    @pl.when(slot == pl.num_programs(0) - 1)
    def _():
        lo_ref[:own_blocks] = acc_ref[...].astype(lo_ref.dtype)
        lo_ref[own_blocks:] = hi_ref[:own_blocks]


def _contract_kernel(left_ref, right_ref, count_ref, *refs):
    out_ref = refs[-1]
    groups = refs[:-1]
    chunks = len(groups) // 3
    slot = pl.program_id(0)
    live = slot < count_ref[0]
    own_blocks = groups[0].shape[0]

    @pl.when(live)
    def _():
        left = left_ref[slot]
        right = right_ref[slot]
        group = right // own_blocks
        index = right % own_blocks
        total = None
        for c in range(chunks):
            own_ref, near_ref, far_ref = groups[3 * c : 3 * c + 3]
            left_rows = own_ref[left]
            right_rows = jnp.where(
                group == 0, own_ref[index], jnp.where(group == 1, near_ref[index], far_ref[index])
            )
            for p in range(left_rows.shape[0]):
                part = lax.dot_general(
                    left_rows[p], right_rows[p], (((1,), (1,)), ((), ())),
                    preferred_element_type=jnp.float32,
                )
                total = part if total is None else total + part
        out_ref[:, 0] = total.reshape(
            out_ref.shape[0], out_ref.shape[2], out_ref.shape[3]
        ).astype(out_ref.dtype)

    @pl.when(jnp.logical_not(live))
    def _():
        out_ref[...] = jnp.zeros_like(out_ref)


CHUNKS = 1


def on_device(pair_list, pair_count, tiles, coeff):
    pair_slots = pair_list.shape[0]
    aux_local = tiles.shape[1]
    block_size = tiles.shape[2]
    orbitals = coeff.shape[1]
    own_blocks = coeff.shape[0] // block_size
    window_blocks = (BAND + 1) * own_blocks
    width = orbitals // CHUNKS
    devices = lax.axis_size("ao")
    owner_index = lax.axis_index("ao")
    first_block = owner_index * own_blocks
    left_rel = (pair_list[:, 0] - first_block).astype(jnp.int32)
    right_rel = (pair_list[:, 1] - first_block).astype(jnp.int32)
    count = pair_count.astype(jnp.int32)
    own_coeff = coeff.reshape(own_blocks, block_size, orbitals)
    ahead_coeff = [passed_along(own_coeff, "ao", -distance) for distance in range(1, BAND + 1)]

    def tile_map(slot, left, right, cnt):
        return (jnp.minimum(slot, jnp.maximum(cnt[0] - 1, 0)), 0, 0, 0)

    def fixed(shape):
        return pl.BlockSpec(shape, lambda s, l, r, c: (0,) * len(shape))

    tile_spec = pl.BlockSpec((1, aux_local, block_size, block_size), tile_map)
    own_shape = (own_blocks, aux_local, block_size, orbitals)
    wide_shape = (2 * own_blocks, aux_local, block_size, orbitals)
    params = pltpu.CompilerParams(
        dimension_semantics=("arbitrary",), vmem_limit_bytes=48 * 1024 * 1024
    )
    hi, part = pl.pallas_call(
        _right_kernel,
        grid_spec=pltpu.PrefetchScalarGridSpec(
            num_scalar_prefetch=3,
            grid=(pair_slots,),
            in_specs=[tile_spec, fixed((own_blocks, block_size, orbitals))],
            out_specs=[fixed(wide_shape), fixed(own_shape)],
            scratch_shapes=[pltpu.VMEM((window_blocks,) + own_shape[1:], jnp.float32)],
        ),
        out_shape=[
            jax.ShapeDtypeStruct(wide_shape, jnp.bfloat16),
            jax.ShapeDtypeStruct(own_shape, jnp.float32),
        ],
        compiler_params=params,
    )(left_rel, right_rel, count, tiles, own_coeff)
    window_coeff = jnp.concatenate([own_coeff] + ahead_coeff, 0)
    lo = pl.pallas_call(
        _left_kernel,
        grid_spec=pltpu.PrefetchScalarGridSpec(
            num_scalar_prefetch=3,
            grid=(pair_slots,),
            in_specs=[
                tile_spec,
                fixed((window_blocks, block_size, orbitals)),
                fixed(own_shape),
                fixed(wide_shape),
            ],
            out_specs=fixed(wide_shape),
            scratch_shapes=[pltpu.VMEM(own_shape, jnp.float32)],
        ),
        out_shape=jax.ShapeDtypeStruct(wide_shape, jnp.bfloat16),
        compiler_params=params,
    )(left_rel, right_rel, count, tiles, window_coeff, part, hi)

    block_shape = own_shape
    nb = own_blocks
    is_even = (owner_index % 2) == 0
    even_up = [(s, s + 1) for s in range(0, devices - 1, 2)]
    odd_down = [(s, s - 1) for s in range(1, devices, 2)]
    odd_up = [(s, s + 1) for s in range(1, devices - 1, 2)]
    even_down = [(s, s - 1) for s in range(2, devices, 2)]

    def f32(value):
        return value.astype(jnp.float32)

    def bf16(value):
        return value.astype(jnp.bfloat16)

    mate_behind = lax.ppermute(hi, "ao", even_up)
    mate_ahead = lax.ppermute(lo, "ao", odd_down)
    up_package = jnp.concatenate([bf16(f32(mate_behind[nb:]) + f32(hi[:nb])), hi[nb:]], 0)
    down_package = jnp.concatenate([lo[:nb], bf16(f32(hi[:nb]) + f32(mate_ahead[:nb]))], 0)
    from_behind = lax.ppermute(up_package, "ao", odd_up)
    from_ahead = lax.ppermute(down_package, "ao", even_down)
    relay_behind = lax.ppermute(from_behind[nb:], "ao", even_up)
    relay_ahead = lax.ppermute(from_ahead[:nb], "ao", odd_down)

    def even_sums(_):
        return (
            bf16(f32(from_behind[:nb]) + f32(lo[:nb])),
            bf16((f32(from_behind[nb:]) + f32(hi[:nb])) + f32(mate_ahead[:nb])),
            bf16((f32(hi[nb:]) + f32(mate_ahead[nb:])) + f32(relay_ahead)),
        )

    def odd_sums(_):
        return (
            bf16((f32(relay_behind) + f32(mate_behind[:nb])) + f32(lo[:nb])),
            bf16((f32(mate_behind[nb:]) + f32(hi[:nb])) + f32(from_ahead[:nb])),
            bf16(f32(hi[nb:]) + f32(from_ahead[nb:])),
        )

    pieces = list(lax.cond(is_even, even_sums, odd_sums, None))
    aux_devices = lax.axis_size("aux")
    share = block_size // aux_devices
    whole = pl.BlockSpec(block_shape, lambda s, l, r, n: (0, 0, 0, 0))
    partial_tiles = pl.pallas_call(
        _contract_kernel,
        grid_spec=pltpu.PrefetchScalarGridSpec(
            num_scalar_prefetch=3,
            grid=(pair_slots,),
            in_specs=[whole] * len(pieces),
            out_specs=pl.BlockSpec(
                (aux_devices, 1, share, block_size), lambda s, l, r, n: (0, s, 0, 0)
            ),
        ),
        out_shape=jax.ShapeDtypeStruct(
            (aux_devices, pair_slots, share, block_size), jnp.bfloat16
        ),
        compiler_params=pltpu.CompilerParams(
            dimension_semantics=("arbitrary",), vmem_limit_bytes=48 * 1024 * 1024
        ),
    )(left_rel, right_rel, count, *pieces)

    gathered = lax.all_to_all(partial_tiles, "aux", 0, 0, tiled=True)
    summed = gathered[0].astype(jnp.float32)
    for source in range(1, aux_devices):
        summed = summed + gathered[source].astype(jnp.float32)
    norm_factor = (aux_local * lax.axis_size("aux") * orbitals) ** (-0.5)
    return (summed * norm_factor).astype(jnp.bfloat16)


def solution(mesh):
    in_specs = (P("ao", None), P("ao"), P("ao", "aux", None, None), P("ao", None))
    out_specs = P("ao", "aux", None)
    return jax.shard_map(
        on_device, mesh=mesh, in_specs=in_specs, out_specs=out_specs, check_vma=False
    )
```

```python
import jax
import jax.numpy as jnp
from jax import lax
from jax.experimental import pallas as pl
from jax.experimental.pallas import tpu as pltpu
from jax.sharding import PartitionSpec as P

BAND = 2


def passed_along(value, axis, steps):
    count = lax.axis_size(axis)
    first, last = (max(0, -steps), min(count, count - steps))
    return lax.ppermute(value, axis, [(source, source + steps) for source in range(first, last)])


def _right_kernel(left_ref, right_ref, count_ref, tile_ref, coeff_ref, hi_ref, part_ref, acc_ref):
    slot = pl.program_id(0)
    own_blocks = part_ref.shape[0]

    @pl.when(slot == 0)
    def _():
        acc_ref[...] = jnp.zeros_like(acc_ref)

    @pl.when(slot < count_ref[0])
    def _():
        tile = tile_ref[0]
        left_coeff = coeff_ref[left_ref[slot]]
        parts = [
            lax.dot_general(
                tile[p], left_coeff, (((0,), (0,)), ((), ())),
                preferred_element_type=jnp.float32,
            )
            for p in range(tile.shape[0])
        ]
        right = right_ref[slot]
        acc_ref[right] += jnp.stack(parts, 0)

    @pl.when(slot == pl.num_programs(0) - 1)
    def _():
        part_ref[...] = acc_ref[:own_blocks]
        width = hi_ref.shape[-1]
        for c in range(hi_ref.shape[0]):
            hi_ref[c] = acc_ref[own_blocks:, :, :, c * width : (c + 1) * width].astype(hi_ref.dtype)


def _left_kernel(left_ref, right_ref, count_ref, tile_ref, coeff_ref, part_ref, hi_ref, lo_ref, acc_ref):
    slot = pl.program_id(0)
    own_blocks = part_ref.shape[0]

    @pl.when(slot == 0)
    def _():
        acc_ref[...] = part_ref[...]

    @pl.when(slot < count_ref[0])
    def _():
        tile = tile_ref[0]
        aux_local, block_size, _ = tile.shape
        to_left = jnp.dot(
            tile.reshape(aux_local * block_size, block_size),
            coeff_ref[right_ref[slot]],
            preferred_element_type=jnp.float32,
        ).reshape(aux_local, block_size, -1)
        left = left_ref[slot]
        acc_ref[left] += to_left

    @pl.when(slot == pl.num_programs(0) - 1)
    def _():
        width = lo_ref.shape[-1]
        for c in range(lo_ref.shape[0]):
            lo_ref[c, :own_blocks] = acc_ref[:, :, :, c * width : (c + 1) * width].astype(lo_ref.dtype)
            lo_ref[c, own_blocks:] = hi_ref[c, :own_blocks]


def _contract_kernel(left_ref, right_ref, count_ref, *refs):
    out_ref = refs[-1]
    groups = refs[:-1]
    chunks = len(groups) // 3
    slot = pl.program_id(0)
    live = slot < count_ref[0]
    own_blocks = groups[0].shape[0]

    @pl.when(live)
    def _():
        left = left_ref[slot]
        right = right_ref[slot]
        group = right // own_blocks
        index = right % own_blocks
        total = None
        for c in range(chunks):
            own_ref, near_ref, far_ref = groups[3 * c : 3 * c + 3]
            left_rows = own_ref[left]
            right_rows = jnp.where(
                group == 0, own_ref[index], jnp.where(group == 1, near_ref[index], far_ref[index])
            )
            for p in range(left_rows.shape[0]):
                part = lax.dot_general(
                    left_rows[p], right_rows[p], (((1,), (1,)), ((), ())),
                    preferred_element_type=jnp.float32,
                )
                total = part if total is None else total + part
        out_ref[:, 0] = total.reshape(
            out_ref.shape[0], out_ref.shape[2], out_ref.shape[3]
        ).astype(out_ref.dtype)

    @pl.when(jnp.logical_not(live))
    def _():
        out_ref[...] = jnp.zeros_like(out_ref)


CHUNKS = 2


def on_device(pair_list, pair_count, tiles, coeff):
    pair_slots = pair_list.shape[0]
    aux_local = tiles.shape[1]
    block_size = tiles.shape[2]
    orbitals = coeff.shape[1]
    own_blocks = coeff.shape[0] // block_size
    window_blocks = (BAND + 1) * own_blocks
    width = orbitals // CHUNKS
    devices = lax.axis_size("ao")
    owner_index = lax.axis_index("ao")
    first_block = owner_index * own_blocks
    left_rel = (pair_list[:, 0] - first_block).astype(jnp.int32)
    right_rel = (pair_list[:, 1] - first_block).astype(jnp.int32)
    count = pair_count.astype(jnp.int32)
    own_coeff = coeff.reshape(own_blocks, block_size, orbitals)
    ahead_coeff = [passed_along(own_coeff, "ao", -distance) for distance in range(1, BAND + 1)]

    def tile_map(slot, left, right, cnt):
        return (jnp.minimum(slot, jnp.maximum(cnt[0] - 1, 0)), 0, 0, 0)

    def fixed(shape):
        return pl.BlockSpec(shape, lambda s, l, r, c: (0,) * len(shape))

    tile_spec = pl.BlockSpec((1, aux_local, block_size, block_size), tile_map)
    own_shape = (own_blocks, aux_local, block_size, orbitals)
    wide_shape = (CHUNKS, 2 * own_blocks, aux_local, block_size, width)
    params = pltpu.CompilerParams(
        dimension_semantics=("arbitrary",), vmem_limit_bytes=48 * 1024 * 1024
    )
    hi, part = pl.pallas_call(
        _right_kernel,
        grid_spec=pltpu.PrefetchScalarGridSpec(
            num_scalar_prefetch=3,
            grid=(pair_slots,),
            in_specs=[tile_spec, fixed((own_blocks, block_size, orbitals))],
            out_specs=[fixed(wide_shape), fixed(own_shape)],
            scratch_shapes=[pltpu.VMEM((window_blocks,) + own_shape[1:], jnp.float32)],
        ),
        out_shape=[
            jax.ShapeDtypeStruct(wide_shape, jnp.bfloat16),
            jax.ShapeDtypeStruct(own_shape, jnp.float32),
        ],
        compiler_params=params,
    )(left_rel, right_rel, count, tiles, own_coeff)
    window_coeff = jnp.concatenate([own_coeff] + ahead_coeff, 0)
    lo = pl.pallas_call(
        _left_kernel,
        grid_spec=pltpu.PrefetchScalarGridSpec(
            num_scalar_prefetch=3,
            grid=(pair_slots,),
            in_specs=[
                tile_spec,
                fixed((window_blocks, block_size, orbitals)),
                fixed(own_shape),
                fixed(wide_shape),
            ],
            out_specs=fixed(wide_shape),
            scratch_shapes=[pltpu.VMEM(own_shape, jnp.float32)],
        ),
        out_shape=jax.ShapeDtypeStruct(wide_shape, jnp.bfloat16),
        compiler_params=params,
    )(left_rel, right_rel, count, tiles, window_coeff, part, hi)

    block_shape = (own_blocks, aux_local, block_size, width)
    is_even = (owner_index % 2) == 0
    even_up_two = [(s, s + 2) for s in range(0, devices - 2, 2)]
    odd_down_two = [(s, s - 2) for s in range(3, devices, 2)]
    even_up_one = [(s, s + 1) for s in range(0, devices - 1, 2)]
    odd_down_one = [(s, s - 1) for s in range(1, devices, 2)]
    pieces = []
    hi_next, lo_next = hi[0], lo[0]
    for c in range(CHUNKS):
        hi_c, lo_c = hi_next, lo_next
        behind_one = passed_along(hi_c, "ao", 1)
        even_two = lax.ppermute(hi_c[own_blocks:], "ao", even_up_two)
        ahead_one = passed_along(lo_c, "ao", -1)
        odd_two = lax.ppermute(lo_c[:own_blocks], "ao", odd_down_two)
        if c + 1 < CHUNKS:
            behind_one, even_two, ahead_one, odd_two, hi_next, lo_next = lax.optimization_barrier(
                (behind_one, even_two, ahead_one, odd_two, hi[c + 1], lo[c + 1])
            )
        relay_behind = lax.ppermute(behind_one[own_blocks:], "ao", even_up_one)
        relay_ahead = lax.ppermute(ahead_one[:own_blocks], "ao", odd_down_one)
        behind_two = jnp.where(is_even, even_two, relay_behind)
        ahead_two = jnp.where(is_even, relay_ahead, odd_two)

        def owner_sum(first, second, third):
            total = first.astype(jnp.float32) + second.astype(jnp.float32)
            return (total + third.astype(jnp.float32)).astype(jnp.bfloat16)

        pieces += [
            owner_sum(behind_two, behind_one[:own_blocks], lo_c[:own_blocks]),
            owner_sum(behind_one[own_blocks:], hi_c[:own_blocks], ahead_one[:own_blocks]),
            owner_sum(hi_c[own_blocks:], ahead_one[own_blocks:], ahead_two),
        ]
    aux_devices = lax.axis_size("aux")
    share = block_size // aux_devices
    whole = pl.BlockSpec(block_shape, lambda s, l, r, n: (0, 0, 0, 0))
    partial_tiles = pl.pallas_call(
        _contract_kernel,
        grid_spec=pltpu.PrefetchScalarGridSpec(
            num_scalar_prefetch=3,
            grid=(pair_slots,),
            in_specs=[whole] * len(pieces),
            out_specs=pl.BlockSpec(
                (aux_devices, 1, share, block_size), lambda s, l, r, n: (0, s, 0, 0)
            ),
        ),
        out_shape=jax.ShapeDtypeStruct(
            (aux_devices, pair_slots, share, block_size), jnp.bfloat16
        ),
        compiler_params=pltpu.CompilerParams(
            dimension_semantics=("arbitrary",), vmem_limit_bytes=48 * 1024 * 1024
        ),
    )(left_rel, right_rel, count, *pieces)

    gathered = lax.all_to_all(partial_tiles, "aux", 0, 0, tiled=True)
    summed = gathered[0].astype(jnp.float32)
    for source in range(1, aux_devices):
        summed = summed + gathered[source].astype(jnp.float32)
    norm_factor = (aux_local * lax.axis_size("aux") * orbitals) ** (-0.5)
    return (summed * norm_factor).astype(jnp.bfloat16)


def solution(mesh):
    in_specs = (P("ao", None), P("ao"), P("ao", "aux", None, None), P("ao", None))
    out_specs = P("ao", "aux", None)
    return jax.shard_map(
        on_device, mesh=mesh, in_specs=in_specs, out_specs=out_specs, check_vma=False
    )
```

```python
import jax
import jax.numpy as jnp
from jax import lax
from jax.experimental import pallas as pl
from jax.experimental.pallas import tpu as pltpu
from jax.sharding import PartitionSpec as P

BAND = 2


def passed_along(value, axis, steps):
    count = lax.axis_size(axis)
    first, last = (max(0, -steps), min(count, count - steps))
    return lax.ppermute(value, axis, [(source, source + steps) for source in range(first, last)])


def _right_kernel(left_ref, right_ref, count_ref, tile_ref, coeff_ref, hi_ref, part_ref, acc_ref):
    slot = pl.program_id(0)
    own_blocks = part_ref.shape[0]

    @pl.when(slot == 0)
    def _():
        acc_ref[...] = jnp.zeros_like(acc_ref)

    @pl.when(slot < count_ref[0])
    def _():
        tile = tile_ref[0]
        left_coeff = coeff_ref[left_ref[slot]]
        parts = [
            lax.dot_general(
                tile[p], left_coeff, (((0,), (0,)), ((), ())),
                preferred_element_type=jnp.float32,
            )
            for p in range(tile.shape[0])
        ]
        right = right_ref[slot]
        acc_ref[right] += jnp.stack(parts, 0)

    @pl.when(slot == pl.num_programs(0) - 1)
    def _():
        part_ref[...] = acc_ref[:own_blocks]
        hi_ref[...] = acc_ref[own_blocks:].astype(hi_ref.dtype)


def _left_kernel(left_ref, right_ref, count_ref, tile_ref, coeff_ref, part_ref, hi_ref, lo_ref, acc_ref):
    slot = pl.program_id(0)
    own_blocks = part_ref.shape[0]

    @pl.when(slot == 0)
    def _():
        acc_ref[...] = part_ref[...]

    @pl.when(slot < count_ref[0])
    def _():
        tile = tile_ref[0]
        aux_local, block_size, _ = tile.shape
        to_left = jnp.dot(
            tile.reshape(aux_local * block_size, block_size),
            coeff_ref[right_ref[slot]],
            preferred_element_type=jnp.float32,
        ).reshape(aux_local, block_size, -1)
        left = left_ref[slot]
        acc_ref[left] += to_left

    @pl.when(slot == pl.num_programs(0) - 1)
    def _():
        lo_ref[:own_blocks] = acc_ref[...].astype(lo_ref.dtype)
        lo_ref[own_blocks:] = hi_ref[:own_blocks]


def _contract_kernel(left_ref, right_ref, count_ref, *refs):
    out_ref = refs[-1]
    groups = refs[:-1]
    chunks = len(groups) // 3
    slot = pl.program_id(0)
    live = slot < count_ref[0]
    own_blocks = groups[0].shape[0]

    @pl.when(live)
    def _():
        left = left_ref[slot]
        right = right_ref[slot]
        group = right // own_blocks
        index = right % own_blocks
        total = None
        for c in range(chunks):
            own_ref, near_ref, far_ref = groups[3 * c : 3 * c + 3]
            left_rows = own_ref[left]
            right_rows = jnp.where(
                group == 0, own_ref[index], jnp.where(group == 1, near_ref[index], far_ref[index])
            )
            for p in range(left_rows.shape[0]):
                part = lax.dot_general(
                    left_rows[p], right_rows[p], (((1,), (1,)), ((), ())),
                    preferred_element_type=jnp.float32,
                )
                total = part if total is None else total + part
        out_ref[:, 0] = total.reshape(
            out_ref.shape[0], out_ref.shape[2], out_ref.shape[3]
        ).astype(out_ref.dtype)

    @pl.when(jnp.logical_not(live))
    def _():
        out_ref[...] = jnp.zeros_like(out_ref)


CHUNKS = 1


def on_device(pair_list, pair_count, tiles, coeff):
    pair_slots = pair_list.shape[0]
    aux_local = tiles.shape[1]
    block_size = tiles.shape[2]
    orbitals = coeff.shape[1]
    own_blocks = coeff.shape[0] // block_size
    window_blocks = (BAND + 1) * own_blocks
    width = orbitals // CHUNKS
    devices = lax.axis_size("ao")
    owner_index = lax.axis_index("ao")
    first_block = owner_index * own_blocks
    left_rel = (pair_list[:, 0] - first_block).astype(jnp.int32)
    right_rel = (pair_list[:, 1] - first_block).astype(jnp.int32)
    count = pair_count.astype(jnp.int32)
    own_coeff = coeff.reshape(own_blocks, block_size, orbitals)
    ahead_coeff = [passed_along(own_coeff, "ao", -distance) for distance in range(1, BAND + 1)]

    def tile_map(slot, left, right, cnt):
        return (jnp.minimum(slot, jnp.maximum(cnt[0] - 1, 0)), 0, 0, 0)

    def fixed(shape):
        return pl.BlockSpec(shape, lambda s, l, r, c: (0,) * len(shape))

    tile_spec = pl.BlockSpec((1, aux_local, block_size, block_size), tile_map)
    own_shape = (own_blocks, aux_local, block_size, orbitals)
    wide_shape = (2 * own_blocks, aux_local, block_size, orbitals)
    params = pltpu.CompilerParams(
        dimension_semantics=("arbitrary",), vmem_limit_bytes=48 * 1024 * 1024
    )
    hi, part = pl.pallas_call(
        _right_kernel,
        grid_spec=pltpu.PrefetchScalarGridSpec(
            num_scalar_prefetch=3,
            grid=(pair_slots,),
            in_specs=[tile_spec, fixed((own_blocks, block_size, orbitals))],
            out_specs=[fixed(wide_shape), fixed(own_shape)],
            scratch_shapes=[pltpu.VMEM((window_blocks,) + own_shape[1:], jnp.float32)],
        ),
        out_shape=[
            jax.ShapeDtypeStruct(wide_shape, jnp.bfloat16),
            jax.ShapeDtypeStruct(own_shape, jnp.float32),
        ],
        compiler_params=params,
    )(left_rel, right_rel, count, tiles, own_coeff)
    window_coeff = jnp.concatenate([own_coeff] + ahead_coeff, 0)
    lo = pl.pallas_call(
        _left_kernel,
        grid_spec=pltpu.PrefetchScalarGridSpec(
            num_scalar_prefetch=3,
            grid=(pair_slots,),
            in_specs=[
                tile_spec,
                fixed((window_blocks, block_size, orbitals)),
                fixed(own_shape),
                fixed(wide_shape),
            ],
            out_specs=fixed(wide_shape),
            scratch_shapes=[pltpu.VMEM(own_shape, jnp.float32)],
        ),
        out_shape=jax.ShapeDtypeStruct(wide_shape, jnp.bfloat16),
        compiler_params=params,
    )(left_rel, right_rel, count, tiles, window_coeff, part, hi)

    block_shape = own_shape
    is_even = (owner_index % 2) == 0
    even_up_two = [(s, s + 2) for s in range(0, devices - 2, 2)]
    odd_down_two = [(s, s - 2) for s in range(3, devices, 2)]
    even_up_one = [(s, s + 1) for s in range(0, devices - 1, 2)]
    odd_down_one = [(s, s - 1) for s in range(1, devices, 2)]
    pieces = []
    for c in range(1):
        behind_one = passed_along(hi, "ao", 1)
        ahead_one = passed_along(lo, "ao", -1)
        behind_one, ahead_one, hi_tail, lo_head = lax.optimization_barrier(
            (behind_one, ahead_one, hi[own_blocks:], lo[:own_blocks])
        )
        even_two = lax.ppermute(hi_tail, "ao", even_up_two)
        odd_two = lax.ppermute(lo_head, "ao", odd_down_two)
        relay_behind = lax.ppermute(behind_one[own_blocks:], "ao", even_up_one)
        relay_ahead = lax.ppermute(ahead_one[:own_blocks], "ao", odd_down_one)
        behind_two = jnp.where(is_even, even_two, relay_behind)
        ahead_two = jnp.where(is_even, relay_ahead, odd_two)

        def owner_sum(first, second, third):
            total = first.astype(jnp.float32) + second.astype(jnp.float32)
            return (total + third.astype(jnp.float32)).astype(jnp.bfloat16)

        pieces += [
            owner_sum(behind_two, behind_one[:own_blocks], lo[:own_blocks]),
            owner_sum(
                behind_one[own_blocks:], hi[:own_blocks], ahead_one[:own_blocks]
            ),
            owner_sum(hi[own_blocks:], ahead_one[own_blocks:], ahead_two),
        ]
    aux_devices = lax.axis_size("aux")
    share = block_size // aux_devices
    whole = pl.BlockSpec(block_shape, lambda s, l, r, n: (0, 0, 0, 0))
    partial_tiles = pl.pallas_call(
        _contract_kernel,
        grid_spec=pltpu.PrefetchScalarGridSpec(
            num_scalar_prefetch=3,
            grid=(pair_slots,),
            in_specs=[whole] * len(pieces),
            out_specs=pl.BlockSpec(
                (aux_devices, 1, share, block_size), lambda s, l, r, n: (0, s, 0, 0)
            ),
        ),
        out_shape=jax.ShapeDtypeStruct(
            (aux_devices, pair_slots, share, block_size), jnp.bfloat16
        ),
        compiler_params=pltpu.CompilerParams(
            dimension_semantics=("arbitrary",), vmem_limit_bytes=48 * 1024 * 1024
        ),
    )(left_rel, right_rel, count, *pieces)

    gathered = lax.all_to_all(partial_tiles, "aux", 0, 0, tiled=True)
    summed = gathered[0].astype(jnp.float32)
    for source in range(1, aux_devices):
        summed = summed + gathered[source].astype(jnp.float32)
    norm_factor = (aux_local * lax.axis_size("aux") * orbitals) ** (-0.5)
    return (summed * norm_factor).astype(jnp.bfloat16)


def solution(mesh):
    in_specs = (P("ao", None), P("ao"), P("ao", "aux", None, None), P("ao", None))
    out_specs = P("ao", "aux", None)
    return jax.shard_map(
        on_device, mesh=mesh, in_specs=in_specs, out_specs=out_specs, check_vma=False
    )
```

```python
import jax
import jax.numpy as jnp
from jax import lax
from jax.experimental import pallas as pl
from jax.experimental.pallas import tpu as pltpu
from jax.sharding import PartitionSpec as P

BAND = 2


def passed_along(value, axis, steps):
    count = lax.axis_size(axis)
    first, last = (max(0, -steps), min(count, count - steps))
    return lax.ppermute(value, axis, [(source, source + steps) for source in range(first, last)])


def _right_kernel(left_ref, right_ref, count_ref, tile_ref, coeff_ref, hi_ref, part_ref, acc_ref):
    slot = pl.program_id(0)
    own_blocks = part_ref.shape[0]

    @pl.when(slot == 0)
    def _():
        acc_ref[...] = jnp.zeros_like(acc_ref)

    @pl.when(slot < count_ref[0])
    def _():
        tile = tile_ref[0]
        left_coeff = coeff_ref[left_ref[slot]]
        parts = [
            lax.dot_general(
                tile[p], left_coeff, (((0,), (0,)), ((), ())),
                preferred_element_type=jnp.float32,
            )
            for p in range(tile.shape[0])
        ]
        right = right_ref[slot]
        acc_ref[right] += jnp.stack(parts, 0)

    @pl.when(slot == pl.num_programs(0) - 1)
    def _():
        part_ref[...] = acc_ref[:own_blocks]
        hi_ref[...] = acc_ref[own_blocks:].astype(hi_ref.dtype)


def _left_kernel(left_ref, right_ref, count_ref, tile_ref, coeff_ref, part_ref, hi_ref, lo_ref, acc_ref):
    slot = pl.program_id(0)
    own_blocks = part_ref.shape[0]

    @pl.when(slot == 0)
    def _():
        acc_ref[...] = part_ref[...]

    @pl.when(slot < count_ref[0])
    def _():
        tile = tile_ref[0]
        aux_local, block_size, _ = tile.shape
        to_left = jnp.dot(
            tile.reshape(aux_local * block_size, block_size),
            coeff_ref[right_ref[slot]],
            preferred_element_type=jnp.float32,
        ).reshape(aux_local, block_size, -1)
        left = left_ref[slot]
        acc_ref[left] += to_left

    @pl.when(slot == pl.num_programs(0) - 1)
    def _():
        lo_ref[:own_blocks] = acc_ref[...].astype(lo_ref.dtype)
        lo_ref[own_blocks:] = hi_ref[:own_blocks]


def _contract_kernel(left_ref, right_ref, count_ref, *refs):
    out_ref = refs[-1]
    groups = refs[:-1]
    chunks = len(groups) // 3
    slot = pl.program_id(0)
    live = slot < count_ref[0]
    own_blocks = groups[0].shape[0]

    @pl.when(live)
    def _():
        left = left_ref[slot]
        right = right_ref[slot]
        group = right // own_blocks
        index = right % own_blocks
        total = None
        for c in range(chunks):
            own_ref, near_ref, far_ref = groups[3 * c : 3 * c + 3]
            left_rows = own_ref[left]
            right_rows = jnp.where(
                group == 0, own_ref[index], jnp.where(group == 1, near_ref[index], far_ref[index])
            )
            for p in range(left_rows.shape[0]):
                part = lax.dot_general(
                    left_rows[p], right_rows[p], (((1,), (1,)), ((), ())),
                    preferred_element_type=jnp.float32,
                )
                total = part if total is None else total + part
        out_ref[:, 0] = total.reshape(
            out_ref.shape[0], out_ref.shape[2], out_ref.shape[3]
        ).astype(out_ref.dtype)

    @pl.when(jnp.logical_not(live))
    def _():
        out_ref[...] = jnp.zeros_like(out_ref)


CHUNKS = 1


def on_device(pair_list, pair_count, tiles, coeff):
    pair_slots = pair_list.shape[0]
    aux_local = tiles.shape[1]
    block_size = tiles.shape[2]
    orbitals = coeff.shape[1]
    own_blocks = coeff.shape[0] // block_size
    window_blocks = (BAND + 1) * own_blocks
    width = orbitals // CHUNKS
    devices = lax.axis_size("ao")
    owner_index = lax.axis_index("ao")
    first_block = owner_index * own_blocks
    left_rel = (pair_list[:, 0] - first_block).astype(jnp.int32)
    right_rel = (pair_list[:, 1] - first_block).astype(jnp.int32)
    count = pair_count.astype(jnp.int32)
    own_coeff = coeff.reshape(own_blocks, block_size, orbitals)
    ahead_coeff = [passed_along(own_coeff, "ao", -distance) for distance in range(1, BAND + 1)]

    def tile_map(slot, left, right, cnt):
        return (jnp.minimum(slot, jnp.maximum(cnt[0] - 1, 0)), 0, 0, 0)

    def fixed(shape):
        return pl.BlockSpec(shape, lambda s, l, r, c: (0,) * len(shape))

    tile_spec = pl.BlockSpec((1, aux_local, block_size, block_size), tile_map)
    own_shape = (own_blocks, aux_local, block_size, orbitals)
    wide_shape = (2 * own_blocks, aux_local, block_size, orbitals)
    params = pltpu.CompilerParams(
        dimension_semantics=("arbitrary",), vmem_limit_bytes=48 * 1024 * 1024
    )
    hi, part = pl.pallas_call(
        _right_kernel,
        grid_spec=pltpu.PrefetchScalarGridSpec(
            num_scalar_prefetch=3,
            grid=(pair_slots,),
            in_specs=[tile_spec, fixed((own_blocks, block_size, orbitals))],
            out_specs=[fixed(wide_shape), fixed(own_shape)],
            scratch_shapes=[pltpu.VMEM((window_blocks,) + own_shape[1:], jnp.float32)],
        ),
        out_shape=[
            jax.ShapeDtypeStruct(wide_shape, jnp.bfloat16),
            jax.ShapeDtypeStruct(own_shape, jnp.float32),
        ],
        compiler_params=params,
    )(left_rel, right_rel, count, tiles, own_coeff)
    window_coeff = jnp.concatenate([own_coeff] + ahead_coeff, 0)
    lo = pl.pallas_call(
        _left_kernel,
        grid_spec=pltpu.PrefetchScalarGridSpec(
            num_scalar_prefetch=3,
            grid=(pair_slots,),
            in_specs=[
                tile_spec,
                fixed((window_blocks, block_size, orbitals)),
                fixed(own_shape),
                fixed(wide_shape),
            ],
            out_specs=fixed(wide_shape),
            scratch_shapes=[pltpu.VMEM(own_shape, jnp.float32)],
        ),
        out_shape=jax.ShapeDtypeStruct(wide_shape, jnp.bfloat16),
        compiler_params=params,
    )(left_rel, right_rel, count, tiles, window_coeff, part, hi)

    block_shape = own_shape
    is_even = (owner_index % 2) == 0
    even_up_two = [(s, s + 2) for s in range(0, devices - 2, 2)]
    odd_down_two = [(s, s - 2) for s in range(3, devices, 2)]
    even_up_one = [(s, s + 1) for s in range(0, devices - 1, 2)]
    odd_down_one = [(s, s - 1) for s in range(1, devices, 2)]
    pieces = []
    for c in range(1):
        behind_one = passed_along(hi, "ao", 1)
        even_two = lax.ppermute(hi[own_blocks:], "ao", even_up_two)
        ahead_one = passed_along(lo, "ao", -1)
        odd_two = lax.ppermute(lo[:own_blocks], "ao", odd_down_two)
        relay_behind = lax.ppermute(behind_one[own_blocks:], "ao", even_up_one)
        relay_ahead = lax.ppermute(ahead_one[:own_blocks], "ao", odd_down_one)

        def owner_sum(first, second, third):
            total = first.astype(jnp.float32) + second.astype(jnp.float32)
            return (total + third.astype(jnp.float32)).astype(jnp.bfloat16)

        def sums(behind_two, ahead_two):
            return (
                owner_sum(behind_two, behind_one[:own_blocks], lo[:own_blocks]),
                owner_sum(behind_one[own_blocks:], hi[:own_blocks], ahead_one[:own_blocks]),
                owner_sum(hi[own_blocks:], ahead_one[own_blocks:], ahead_two),
            )

        pieces += list(
            lax.cond(
                is_even,
                lambda _: sums(even_two, relay_ahead),
                lambda _: sums(relay_behind, odd_two),
                None,
            )
        )
    aux_devices = lax.axis_size("aux")
    share = block_size // aux_devices
    whole = pl.BlockSpec(block_shape, lambda s, l, r, n: (0, 0, 0, 0))
    partial_tiles = pl.pallas_call(
        _contract_kernel,
        grid_spec=pltpu.PrefetchScalarGridSpec(
            num_scalar_prefetch=3,
            grid=(pair_slots,),
            in_specs=[whole] * len(pieces),
            out_specs=pl.BlockSpec(
                (aux_devices, 1, share, block_size), lambda s, l, r, n: (0, s, 0, 0)
            ),
        ),
        out_shape=jax.ShapeDtypeStruct(
            (aux_devices, pair_slots, share, block_size), jnp.bfloat16
        ),
        compiler_params=pltpu.CompilerParams(
            dimension_semantics=("arbitrary",), vmem_limit_bytes=48 * 1024 * 1024
        ),
    )(left_rel, right_rel, count, *pieces)

    gathered = lax.all_to_all(partial_tiles, "aux", 0, 0, tiled=True)
    summed = gathered[0].astype(jnp.float32)
    for source in range(1, aux_devices):
        summed = summed + gathered[source].astype(jnp.float32)
    norm_factor = (aux_local * lax.axis_size("aux") * orbitals) ** (-0.5)
    return (summed * norm_factor).astype(jnp.bfloat16)


def solution(mesh):
    in_specs = (P("ao", None), P("ao"), P("ao", "aux", None, None), P("ao", None))
    out_specs = P("ao", "aux", None)
    return jax.shard_map(
        on_device, mesh=mesh, in_specs=in_specs, out_specs=out_specs, check_vma=False
    )
```

```python
import jax
import jax.numpy as jnp
from jax import lax
from jax.experimental import pallas as pl
from jax.experimental.pallas import tpu as pltpu
from jax.sharding import PartitionSpec as P

BAND = 2


def passed_along(value, axis, steps):
    count = lax.axis_size(axis)
    first, last = (max(0, -steps), min(count, count - steps))
    return lax.ppermute(value, axis, [(source, source + steps) for source in range(first, last)])


def _right_kernel(left_ref, right_ref, count_ref, tile_ref, coeff_ref, near_ref, far_ref, part_ref, acc_ref):
    slot = pl.program_id(0)
    own_blocks = part_ref.shape[0]

    @pl.when(slot == 0)
    def _():
        acc_ref[...] = jnp.zeros_like(acc_ref)

    @pl.when(slot < count_ref[0])
    def _():
        tile = tile_ref[0]
        left_coeff = coeff_ref[left_ref[slot]]
        parts = [
            lax.dot_general(
                tile[p], left_coeff, (((0,), (0,)), ((), ())),
                preferred_element_type=jnp.float32,
            )
            for p in range(tile.shape[0])
        ]
        right = right_ref[slot]
        acc_ref[right] += jnp.stack(parts, 0)

    @pl.when(slot == pl.num_programs(0) - 1)
    def _():
        part_ref[...] = acc_ref[:own_blocks]
        near_ref[...] = acc_ref[own_blocks : 2 * own_blocks].astype(near_ref.dtype)
        far_ref[...] = acc_ref[2 * own_blocks :].astype(far_ref.dtype)


def _left_kernel(left_ref, right_ref, count_ref, tile_ref, coeff_ref, part_ref, lo_ref, acc_ref):
    slot = pl.program_id(0)
    own_blocks = part_ref.shape[0]

    @pl.when(slot == 0)
    def _():
        acc_ref[...] = part_ref[...]

    @pl.when(slot < count_ref[0])
    def _():
        tile = tile_ref[0]
        aux_local, block_size, _ = tile.shape
        to_left = jnp.dot(
            tile.reshape(aux_local * block_size, block_size),
            coeff_ref[right_ref[slot]],
            preferred_element_type=jnp.float32,
        ).reshape(aux_local, block_size, -1)
        left = left_ref[slot]
        acc_ref[left] += to_left

    @pl.when(slot == pl.num_programs(0) - 1)
    def _():
        lo_ref[...] = acc_ref[...].astype(lo_ref.dtype)


def _contract_kernel(left_ref, right_ref, count_ref, *refs):
    out_ref = refs[-1]
    groups = refs[:-1]
    chunks = len(groups) // 3
    slot = pl.program_id(0)
    live = slot < count_ref[0]
    own_blocks = groups[0].shape[0]

    @pl.when(live)
    def _():
        left = left_ref[slot]
        right = right_ref[slot]
        group = right // own_blocks
        index = right % own_blocks
        total = None
        for c in range(chunks):
            own_ref, near_ref, far_ref = groups[3 * c : 3 * c + 3]
            left_rows = own_ref[left]
            right_rows = jnp.where(
                group == 0, own_ref[index], jnp.where(group == 1, near_ref[index], far_ref[index])
            )
            for p in range(left_rows.shape[0]):
                part = lax.dot_general(
                    left_rows[p], right_rows[p], (((1,), (1,)), ((), ())),
                    preferred_element_type=jnp.float32,
                )
                total = part if total is None else total + part
        out_ref[:, 0] = total.reshape(
            out_ref.shape[0], out_ref.shape[2], out_ref.shape[3]
        ).astype(out_ref.dtype)

    @pl.when(jnp.logical_not(live))
    def _():
        out_ref[...] = jnp.zeros_like(out_ref)


CHUNKS = 1


def on_device(pair_list, pair_count, tiles, coeff):
    pair_slots = pair_list.shape[0]
    aux_local = tiles.shape[1]
    block_size = tiles.shape[2]
    orbitals = coeff.shape[1]
    own_blocks = coeff.shape[0] // block_size
    window_blocks = (BAND + 1) * own_blocks
    width = orbitals // CHUNKS
    devices = lax.axis_size("ao")
    owner_index = lax.axis_index("ao")
    first_block = owner_index * own_blocks
    left_rel = (pair_list[:, 0] - first_block).astype(jnp.int32)
    right_rel = (pair_list[:, 1] - first_block).astype(jnp.int32)
    count = pair_count.astype(jnp.int32)
    own_coeff = coeff.reshape(own_blocks, block_size, orbitals)
    ahead_coeff = [passed_along(own_coeff, "ao", -distance) for distance in range(1, BAND + 1)]

    def tile_map(slot, left, right, cnt):
        return (jnp.minimum(slot, jnp.maximum(cnt[0] - 1, 0)), 0, 0, 0)

    def fixed(shape):
        return pl.BlockSpec(shape, lambda s, l, r, c: (0,) * len(shape))

    tile_spec = pl.BlockSpec((1, aux_local, block_size, block_size), tile_map)
    own_shape = (own_blocks, aux_local, block_size, orbitals)
    wide_shape = (2 * own_blocks, aux_local, block_size, orbitals)
    params = pltpu.CompilerParams(
        dimension_semantics=("arbitrary",), vmem_limit_bytes=48 * 1024 * 1024
    )
    hi_near, hi_far, part = pl.pallas_call(
        _right_kernel,
        grid_spec=pltpu.PrefetchScalarGridSpec(
            num_scalar_prefetch=3,
            grid=(pair_slots,),
            in_specs=[tile_spec, fixed((own_blocks, block_size, orbitals))],
            out_specs=[fixed(own_shape), fixed(own_shape), fixed(own_shape)],
            scratch_shapes=[pltpu.VMEM((window_blocks,) + own_shape[1:], jnp.float32)],
        ),
        out_shape=[
            jax.ShapeDtypeStruct(own_shape, jnp.bfloat16),
            jax.ShapeDtypeStruct(own_shape, jnp.bfloat16),
            jax.ShapeDtypeStruct(own_shape, jnp.float32),
        ],
        compiler_params=params,
    )(left_rel, right_rel, count, tiles, own_coeff)
    window_coeff = jnp.concatenate([own_coeff] + ahead_coeff, 0)
    lo = pl.pallas_call(
        _left_kernel,
        grid_spec=pltpu.PrefetchScalarGridSpec(
            num_scalar_prefetch=3,
            grid=(pair_slots,),
            in_specs=[
                tile_spec,
                fixed((window_blocks, block_size, orbitals)),
                fixed(own_shape),
            ],
            out_specs=fixed(own_shape),
            scratch_shapes=[pltpu.VMEM(own_shape, jnp.float32)],
        ),
        out_shape=jax.ShapeDtypeStruct(own_shape, jnp.bfloat16),
        compiler_params=params,
    )(left_rel, right_rel, count, tiles, window_coeff, part)

    block_shape = own_shape
    is_even = (owner_index % 2) == 0
    even_up_two = [(s, s + 2) for s in range(0, devices - 2, 2)]
    odd_down_two = [(s, s - 2) for s in range(3, devices, 2)]
    even_up_one = [(s, s + 1) for s in range(0, devices - 1, 2)]
    odd_down_one = [(s, s - 1) for s in range(1, devices, 2)]
    pieces = []
    for c in range(1):
        behind_near = passed_along(hi_near, "ao", 1)
        behind_far = passed_along(hi_far, "ao", 1)
        even_two = lax.ppermute(hi_far, "ao", even_up_two)
        ahead_own = passed_along(lo, "ao", -1)
        ahead_near = passed_along(hi_near, "ao", -1)
        odd_two = lax.ppermute(lo, "ao", odd_down_two)
        relay_behind = lax.ppermute(behind_far, "ao", even_up_one)
        relay_ahead = lax.ppermute(ahead_own, "ao", odd_down_one)

        def owner_sum(first, second, third):
            total = first.astype(jnp.float32) + second.astype(jnp.float32)
            return (total + third.astype(jnp.float32)).astype(jnp.bfloat16)

        def sums(behind_two, ahead_two):
            return (
                owner_sum(behind_two, behind_near, lo),
                owner_sum(behind_far, hi_near, ahead_own),
                owner_sum(hi_far, ahead_near, ahead_two),
            )

        pieces += list(
            lax.cond(
                is_even,
                lambda _: sums(even_two, relay_ahead),
                lambda _: sums(relay_behind, odd_two),
                None,
            )
        )
    aux_devices = lax.axis_size("aux")
    share = block_size // aux_devices
    whole = pl.BlockSpec(block_shape, lambda s, l, r, n: (0, 0, 0, 0))
    partial_tiles = pl.pallas_call(
        _contract_kernel,
        grid_spec=pltpu.PrefetchScalarGridSpec(
            num_scalar_prefetch=3,
            grid=(pair_slots,),
            in_specs=[whole] * len(pieces),
            out_specs=pl.BlockSpec(
                (aux_devices, 1, share, block_size), lambda s, l, r, n: (0, s, 0, 0)
            ),
        ),
        out_shape=jax.ShapeDtypeStruct(
            (aux_devices, pair_slots, share, block_size), jnp.bfloat16
        ),
        compiler_params=pltpu.CompilerParams(
            dimension_semantics=("arbitrary",), vmem_limit_bytes=48 * 1024 * 1024
        ),
    )(left_rel, right_rel, count, *pieces)

    gathered = lax.all_to_all(partial_tiles, "aux", 0, 0, tiled=True)
    summed = gathered[0].astype(jnp.float32)
    for source in range(1, aux_devices):
        summed = summed + gathered[source].astype(jnp.float32)
    norm_factor = (aux_local * lax.axis_size("aux") * orbitals) ** (-0.5)
    return (summed * norm_factor).astype(jnp.bfloat16)


def solution(mesh):
    in_specs = (P("ao", None), P("ao"), P("ao", "aux", None, None), P("ao", None))
    out_specs = P("ao", "aux", None)
    return jax.shard_map(
        on_device, mesh=mesh, in_specs=in_specs, out_specs=out_specs, check_vma=False
    )
```

```python
import jax
import jax.numpy as jnp
from jax import lax
from jax.experimental import pallas as pl
from jax.experimental.pallas import tpu as pltpu
from jax.sharding import PartitionSpec as P

BAND = 2


def passed_along(value, axis, steps):
    count = lax.axis_size(axis)
    first, last = (max(0, -steps), min(count, count - steps))
    return lax.ppermute(value, axis, [(source, source + steps) for source in range(first, last)])


def _right_kernel(left_ref, right_ref, count_ref, tile_ref, coeff_ref, near_ref, far_ref, part_ref, acc_ref):
    slot = pl.program_id(0)
    own_blocks = part_ref.shape[0]

    @pl.when(slot == 0)
    def _():
        acc_ref[...] = jnp.zeros_like(acc_ref)

    @pl.when(slot < count_ref[0])
    def _():
        tile = tile_ref[0]
        left_coeff = coeff_ref[left_ref[slot]]
        parts = [
            lax.dot_general(
                tile[p], left_coeff, (((0,), (0,)), ((), ())),
                preferred_element_type=jnp.float32,
            )
            for p in range(tile.shape[0])
        ]
        right = right_ref[slot]
        acc_ref[right] += jnp.stack(parts, 0)

    @pl.when(slot == pl.num_programs(0) - 1)
    def _():
        part_ref[...] = acc_ref[:own_blocks]
        near_ref[...] = acc_ref[own_blocks : 2 * own_blocks].astype(near_ref.dtype)
        far_ref[...] = acc_ref[2 * own_blocks :].astype(far_ref.dtype)


def _left_kernel(left_ref, right_ref, count_ref, tile_ref, own_ref, near_ref, far_ref, part_ref, lo_ref, acc_ref):
    slot = pl.program_id(0)
    own_blocks = part_ref.shape[0]

    @pl.when(slot == 0)
    def _():
        acc_ref[...] = part_ref[...]

    @pl.when(slot < count_ref[0])
    def _():
        tile = tile_ref[0]
        aux_local, block_size, _ = tile.shape
        right = right_ref[slot]
        group = right // own_ref.shape[0]
        index = right % own_ref.shape[0]
        right_coeff = jnp.where(
            group == 0, own_ref[index], jnp.where(group == 1, near_ref[index], far_ref[index])
        )
        to_left = jnp.dot(
            tile.reshape(aux_local * block_size, block_size),
            right_coeff,
            preferred_element_type=jnp.float32,
        ).reshape(aux_local, block_size, -1)
        left = left_ref[slot]
        acc_ref[left] += to_left

    @pl.when(slot == pl.num_programs(0) - 1)
    def _():
        lo_ref[...] = acc_ref[...].astype(lo_ref.dtype)


def _contract_kernel(left_ref, right_ref, count_ref, *refs):
    out_ref = refs[-1]
    groups = refs[:-1]
    chunks = len(groups) // 3
    slot = pl.program_id(0)
    live = slot < count_ref[0]
    own_blocks = groups[0].shape[0]

    @pl.when(live)
    def _():
        left = left_ref[slot]
        right = right_ref[slot]
        group = right // own_blocks
        index = right % own_blocks
        total = None
        for c in range(chunks):
            own_ref, near_ref, far_ref = groups[3 * c : 3 * c + 3]
            left_rows = own_ref[left]
            right_rows = jnp.where(
                group == 0, own_ref[index], jnp.where(group == 1, near_ref[index], far_ref[index])
            )
            for p in range(left_rows.shape[0]):
                part = lax.dot_general(
                    left_rows[p], right_rows[p], (((1,), (1,)), ((), ())),
                    preferred_element_type=jnp.float32,
                )
                total = part if total is None else total + part
        out_ref[:, 0] = total.reshape(
            out_ref.shape[0], out_ref.shape[2], out_ref.shape[3]
        ).astype(out_ref.dtype)

    @pl.when(jnp.logical_not(live))
    def _():
        out_ref[...] = jnp.zeros_like(out_ref)


CHUNKS = 1


def on_device(pair_list, pair_count, tiles, coeff):
    pair_slots = pair_list.shape[0]
    aux_local = tiles.shape[1]
    block_size = tiles.shape[2]
    orbitals = coeff.shape[1]
    own_blocks = coeff.shape[0] // block_size
    window_blocks = (BAND + 1) * own_blocks
    width = orbitals // CHUNKS
    devices = lax.axis_size("ao")
    owner_index = lax.axis_index("ao")
    first_block = owner_index * own_blocks
    left_rel = (pair_list[:, 0] - first_block).astype(jnp.int32)
    right_rel = (pair_list[:, 1] - first_block).astype(jnp.int32)
    count = pair_count.astype(jnp.int32)
    own_coeff = coeff.reshape(own_blocks, block_size, orbitals)
    ahead_coeff = [passed_along(own_coeff, "ao", -distance) for distance in range(1, BAND + 1)]

    def tile_map(slot, left, right, cnt):
        return (jnp.minimum(slot, jnp.maximum(cnt[0] - 1, 0)), 0, 0, 0)

    def fixed(shape):
        return pl.BlockSpec(shape, lambda s, l, r, c: (0,) * len(shape))

    tile_spec = pl.BlockSpec((1, aux_local, block_size, block_size), tile_map)
    own_shape = (own_blocks, aux_local, block_size, orbitals)
    wide_shape = (2 * own_blocks, aux_local, block_size, orbitals)
    params = pltpu.CompilerParams(
        dimension_semantics=("arbitrary",), vmem_limit_bytes=48 * 1024 * 1024
    )
    hi_near, hi_far, part = pl.pallas_call(
        _right_kernel,
        grid_spec=pltpu.PrefetchScalarGridSpec(
            num_scalar_prefetch=3,
            grid=(pair_slots,),
            in_specs=[tile_spec, fixed((own_blocks, block_size, orbitals))],
            out_specs=[fixed(own_shape), fixed(own_shape), fixed(own_shape)],
            scratch_shapes=[pltpu.VMEM((window_blocks,) + own_shape[1:], jnp.float32)],
        ),
        out_shape=[
            jax.ShapeDtypeStruct(own_shape, jnp.bfloat16),
            jax.ShapeDtypeStruct(own_shape, jnp.bfloat16),
            jax.ShapeDtypeStruct(own_shape, jnp.float32),
        ],
        compiler_params=params,
    )(left_rel, right_rel, count, tiles, own_coeff)
    lo = pl.pallas_call(
        _left_kernel,
        grid_spec=pltpu.PrefetchScalarGridSpec(
            num_scalar_prefetch=3,
            grid=(pair_slots,),
            in_specs=[
                tile_spec,
                fixed((own_blocks, block_size, orbitals)),
                fixed((own_blocks, block_size, orbitals)),
                fixed((own_blocks, block_size, orbitals)),
                fixed(own_shape),
            ],
            out_specs=fixed(own_shape),
            scratch_shapes=[pltpu.VMEM(own_shape, jnp.float32)],
        ),
        out_shape=jax.ShapeDtypeStruct(own_shape, jnp.bfloat16),
        compiler_params=params,
    )(left_rel, right_rel, count, tiles, own_coeff, *ahead_coeff, part)

    block_shape = own_shape
    is_even = (owner_index % 2) == 0
    even_up_two = [(s, s + 2) for s in range(0, devices - 2, 2)]
    odd_down_two = [(s, s - 2) for s in range(3, devices, 2)]
    even_up_one = [(s, s + 1) for s in range(0, devices - 1, 2)]
    odd_down_one = [(s, s - 1) for s in range(1, devices, 2)]
    pieces = []
    for c in range(1):
        behind_near = passed_along(hi_near, "ao", 1)
        behind_far = passed_along(hi_far, "ao", 1)
        even_two = lax.ppermute(hi_far, "ao", even_up_two)
        ahead_own = passed_along(lo, "ao", -1)
        ahead_near = passed_along(hi_near, "ao", -1)
        odd_two = lax.ppermute(lo, "ao", odd_down_two)
        relay_behind = lax.ppermute(behind_far, "ao", even_up_one)
        relay_ahead = lax.ppermute(ahead_own, "ao", odd_down_one)

        def owner_sum(first, second, third):
            total = first.astype(jnp.float32) + second.astype(jnp.float32)
            return (total + third.astype(jnp.float32)).astype(jnp.bfloat16)

        def sums(behind_two, ahead_two):
            return (
                owner_sum(behind_two, behind_near, lo),
                owner_sum(behind_far, hi_near, ahead_own),
                owner_sum(hi_far, ahead_near, ahead_two),
            )

        pieces += list(
            lax.cond(
                is_even,
                lambda _: sums(even_two, relay_ahead),
                lambda _: sums(relay_behind, odd_two),
                None,
            )
        )
    aux_devices = lax.axis_size("aux")
    share = block_size // aux_devices
    whole = pl.BlockSpec(block_shape, lambda s, l, r, n: (0, 0, 0, 0))
    partial_tiles = pl.pallas_call(
        _contract_kernel,
        grid_spec=pltpu.PrefetchScalarGridSpec(
            num_scalar_prefetch=3,
            grid=(pair_slots,),
            in_specs=[whole] * len(pieces),
            out_specs=pl.BlockSpec(
                (aux_devices, 1, share, block_size), lambda s, l, r, n: (0, s, 0, 0)
            ),
        ),
        out_shape=jax.ShapeDtypeStruct(
            (aux_devices, pair_slots, share, block_size), jnp.bfloat16
        ),
        compiler_params=pltpu.CompilerParams(
            dimension_semantics=("arbitrary",), vmem_limit_bytes=48 * 1024 * 1024
        ),
    )(left_rel, right_rel, count, *pieces)

    gathered = lax.all_to_all(partial_tiles, "aux", 0, 0, tiled=True)
    summed = gathered[0].astype(jnp.float32)
    for source in range(1, aux_devices):
        summed = summed + gathered[source].astype(jnp.float32)
    norm_factor = (aux_local * lax.axis_size("aux") * orbitals) ** (-0.5)
    return (summed * norm_factor).astype(jnp.bfloat16)


def solution(mesh):
    in_specs = (P("ao", None), P("ao"), P("ao", "aux", None, None), P("ao", None))
    out_specs = P("ao", "aux", None)
    return jax.shard_map(
        on_device, mesh=mesh, in_specs=in_specs, out_specs=out_specs, check_vma=False
    )
```

```python
import jax
import jax.numpy as jnp
from jax import lax
from jax.experimental import pallas as pl
from jax.experimental.pallas import tpu as pltpu
from jax.sharding import PartitionSpec as P

BAND = 2


def passed_along(value, axis, steps):
    count = lax.axis_size(axis)
    first, last = (max(0, -steps), min(count, count - steps))
    return lax.ppermute(value, axis, [(source, source + steps) for source in range(first, last)])


def _right_kernel(left_ref, right_ref, count_ref, tile_ref, coeff_ref, near_ref, far_ref, part_ref, acc_ref):
    slot = pl.program_id(0)
    own_blocks = part_ref.shape[0]

    @pl.when(slot == 0)
    def _():
        acc_ref[...] = jnp.zeros_like(acc_ref)

    @pl.when(slot < count_ref[0])
    def _():
        tile = tile_ref[0]
        left_coeff = coeff_ref[left_ref[slot]]
        aux_local, block_size, _ = tile.shape
        turned = jnp.swapaxes(tile, 1, 2).reshape(aux_local * block_size, block_size)
        to_right = jnp.dot(turned, left_coeff, preferred_element_type=jnp.float32)
        right = right_ref[slot]
        acc_ref[right] += to_right.reshape(aux_local, block_size, -1)

    @pl.when(slot == pl.num_programs(0) - 1)
    def _():
        part_ref[...] = acc_ref[:own_blocks]
        near_ref[...] = acc_ref[own_blocks : 2 * own_blocks].astype(near_ref.dtype)
        far_ref[...] = acc_ref[2 * own_blocks :].astype(far_ref.dtype)


def _left_kernel(left_ref, right_ref, count_ref, tile_ref, own_ref, near_ref, far_ref, part_ref, lo_ref, acc_ref):
    slot = pl.program_id(0)
    own_blocks = part_ref.shape[0]

    @pl.when(slot == 0)
    def _():
        acc_ref[...] = part_ref[...]

    @pl.when(slot < count_ref[0])
    def _():
        tile = tile_ref[0]
        aux_local, block_size, _ = tile.shape
        right = right_ref[slot]
        group = right // own_ref.shape[0]
        index = right % own_ref.shape[0]
        right_coeff = jnp.where(
            group == 0, own_ref[index], jnp.where(group == 1, near_ref[index], far_ref[index])
        )
        to_left = jnp.dot(
            tile.reshape(aux_local * block_size, block_size),
            right_coeff,
            preferred_element_type=jnp.float32,
        ).reshape(aux_local, block_size, -1)
        left = left_ref[slot]
        acc_ref[left] += to_left

    @pl.when(slot == pl.num_programs(0) - 1)
    def _():
        lo_ref[...] = acc_ref[...].astype(lo_ref.dtype)


def _contract_kernel(left_ref, right_ref, count_ref, *refs):
    out_ref = refs[-1]
    groups = refs[:-1]
    chunks = len(groups) // 3
    slot = pl.program_id(0)
    live = slot < count_ref[0]
    own_blocks = groups[0].shape[0]

    @pl.when(live)
    def _():
        left = left_ref[slot]
        right = right_ref[slot]
        group = right // own_blocks
        index = right % own_blocks
        total = None
        for c in range(chunks):
            own_ref, near_ref, far_ref = groups[3 * c : 3 * c + 3]
            left_rows = own_ref[left]
            right_rows = jnp.where(
                group == 0, own_ref[index], jnp.where(group == 1, near_ref[index], far_ref[index])
            )
            for p in range(left_rows.shape[0]):
                part = lax.dot_general(
                    left_rows[p], right_rows[p], (((1,), (1,)), ((), ())),
                    preferred_element_type=jnp.float32,
                )
                total = part if total is None else total + part
        out_ref[:, 0] = total.reshape(
            out_ref.shape[0], out_ref.shape[2], out_ref.shape[3]
        ).astype(out_ref.dtype)

    @pl.when(jnp.logical_not(live))
    def _():
        out_ref[...] = jnp.zeros_like(out_ref)


CHUNKS = 1


def on_device(pair_list, pair_count, tiles, coeff):
    pair_slots = pair_list.shape[0]
    aux_local = tiles.shape[1]
    block_size = tiles.shape[2]
    orbitals = coeff.shape[1]
    own_blocks = coeff.shape[0] // block_size
    window_blocks = (BAND + 1) * own_blocks
    width = orbitals // CHUNKS
    devices = lax.axis_size("ao")
    owner_index = lax.axis_index("ao")
    first_block = owner_index * own_blocks
    left_rel = (pair_list[:, 0] - first_block).astype(jnp.int32)
    right_rel = (pair_list[:, 1] - first_block).astype(jnp.int32)
    count = pair_count.astype(jnp.int32)
    own_coeff = coeff.reshape(own_blocks, block_size, orbitals)
    ahead_coeff = [passed_along(own_coeff, "ao", -distance) for distance in range(1, BAND + 1)]

    def tile_map(slot, left, right, cnt):
        return (jnp.minimum(slot, jnp.maximum(cnt[0] - 1, 0)), 0, 0, 0)

    def fixed(shape):
        return pl.BlockSpec(shape, lambda s, l, r, c: (0,) * len(shape))

    tile_spec = pl.BlockSpec((1, aux_local, block_size, block_size), tile_map)
    own_shape = (own_blocks, aux_local, block_size, orbitals)
    wide_shape = (2 * own_blocks, aux_local, block_size, orbitals)
    params = pltpu.CompilerParams(
        dimension_semantics=("arbitrary",), vmem_limit_bytes=48 * 1024 * 1024
    )
    hi_near, hi_far, part = pl.pallas_call(
        _right_kernel,
        grid_spec=pltpu.PrefetchScalarGridSpec(
            num_scalar_prefetch=3,
            grid=(pair_slots,),
            in_specs=[tile_spec, fixed((own_blocks, block_size, orbitals))],
            out_specs=[fixed(own_shape), fixed(own_shape), fixed(own_shape)],
            scratch_shapes=[pltpu.VMEM((window_blocks,) + own_shape[1:], jnp.float32)],
        ),
        out_shape=[
            jax.ShapeDtypeStruct(own_shape, jnp.bfloat16),
            jax.ShapeDtypeStruct(own_shape, jnp.bfloat16),
            jax.ShapeDtypeStruct(own_shape, jnp.float32),
        ],
        compiler_params=params,
    )(left_rel, right_rel, count, tiles, own_coeff)
    lo = pl.pallas_call(
        _left_kernel,
        grid_spec=pltpu.PrefetchScalarGridSpec(
            num_scalar_prefetch=3,
            grid=(pair_slots,),
            in_specs=[
                tile_spec,
                fixed((own_blocks, block_size, orbitals)),
                fixed((own_blocks, block_size, orbitals)),
                fixed((own_blocks, block_size, orbitals)),
                fixed(own_shape),
            ],
            out_specs=fixed(own_shape),
            scratch_shapes=[pltpu.VMEM(own_shape, jnp.float32)],
        ),
        out_shape=jax.ShapeDtypeStruct(own_shape, jnp.bfloat16),
        compiler_params=params,
    )(left_rel, right_rel, count, tiles, own_coeff, *ahead_coeff, part)

    block_shape = own_shape
    is_even = (owner_index % 2) == 0
    even_up_two = [(s, s + 2) for s in range(0, devices - 2, 2)]
    odd_down_two = [(s, s - 2) for s in range(3, devices, 2)]
    even_up_one = [(s, s + 1) for s in range(0, devices - 1, 2)]
    odd_down_one = [(s, s - 1) for s in range(1, devices, 2)]
    pieces = []
    for c in range(1):
        behind_near = passed_along(hi_near, "ao", 1)
        behind_far = passed_along(hi_far, "ao", 1)
        even_two = lax.ppermute(hi_far, "ao", even_up_two)
        ahead_own = passed_along(lo, "ao", -1)
        ahead_near = passed_along(hi_near, "ao", -1)
        odd_two = lax.ppermute(lo, "ao", odd_down_two)
        relay_behind = lax.ppermute(behind_far, "ao", even_up_one)
        relay_ahead = lax.ppermute(ahead_own, "ao", odd_down_one)

        def owner_sum(first, second, third):
            total = first.astype(jnp.float32) + second.astype(jnp.float32)
            return (total + third.astype(jnp.float32)).astype(jnp.bfloat16)

        def sums(behind_two, ahead_two):
            return (
                owner_sum(behind_two, behind_near, lo),
                owner_sum(behind_far, hi_near, ahead_own),
                owner_sum(hi_far, ahead_near, ahead_two),
            )

        pieces += list(
            lax.cond(
                is_even,
                lambda _: sums(even_two, relay_ahead),
                lambda _: sums(relay_behind, odd_two),
                None,
            )
        )
    aux_devices = lax.axis_size("aux")
    share = block_size // aux_devices
    whole = pl.BlockSpec(block_shape, lambda s, l, r, n: (0, 0, 0, 0))
    partial_tiles = pl.pallas_call(
        _contract_kernel,
        grid_spec=pltpu.PrefetchScalarGridSpec(
            num_scalar_prefetch=3,
            grid=(pair_slots,),
            in_specs=[whole] * len(pieces),
            out_specs=pl.BlockSpec(
                (aux_devices, 1, share, block_size), lambda s, l, r, n: (0, s, 0, 0)
            ),
        ),
        out_shape=jax.ShapeDtypeStruct(
            (aux_devices, pair_slots, share, block_size), jnp.bfloat16
        ),
        compiler_params=pltpu.CompilerParams(
            dimension_semantics=("arbitrary",), vmem_limit_bytes=48 * 1024 * 1024
        ),
    )(left_rel, right_rel, count, *pieces)

    gathered = lax.all_to_all(partial_tiles, "aux", 0, 0, tiled=True)
    summed = gathered[0].astype(jnp.float32)
    for source in range(1, aux_devices):
        summed = summed + gathered[source].astype(jnp.float32)
    norm_factor = (aux_local * lax.axis_size("aux") * orbitals) ** (-0.5)
    return (summed * norm_factor).astype(jnp.bfloat16)


def solution(mesh):
    in_specs = (P("ao", None), P("ao"), P("ao", "aux", None, None), P("ao", None))
    out_specs = P("ao", "aux", None)
    return jax.shard_map(
        on_device, mesh=mesh, in_specs=in_specs, out_specs=out_specs, check_vma=False
    )
```
